256 devices in a mesh: ctx: 32 (over x, z), tp: 8 (over y, core).
Axes of the slice: x: 4, y: 4, z: 8, core: 2. Of those that a mesh axis runs over, the one named last changes fastest.
Arguments:
- hidden: bfloat16 [8192, 2688], P('ctx', 'tp'), may hold values from -6 to 6
- mamba_x: bfloat16 [8192, 4096], P('ctx', 'tp'), may hold values from -6 to 6
- gate_z: bfloat16 [8192, 4096], P('ctx', 'tp'), may hold values from -6 to 6
- b_input: bfloat16 [8192, 1024], P('ctx', 'tp'), may hold values from -6 to 6
- c_input: bfloat16 [8192, 1024], P('ctx', 'tp'), may hold values from -0.59765625 to 0.59765625
- dt_raw: float32 [8192, 64], P('ctx', 'tp'), may hold values from -5 to 5
- dt_bias: float32 [64], P('tp'), may hold values from -2 to 1
- decay_log: float32 [64], P('tp'), may hold values from -10 to -3
- d_skip: float32 [64], P('tp'), may hold values from 0.5 to 1.5
- mixer_gain: float32 [4096], P('tp'), may hold values from 0.1 to 1.9
- out_weight: bfloat16 [4096, 2688], P('tp'), may hold values from -0.125 to 0.125
- attn_gain: float32 [2688], replicated, may hold values from 0.5 to 12
- w_query: bfloat16 [2688, 4096], P(None, 'tp'), may hold values from -0.125 to 0.125
- w_keyval: bfloat16 [2, 2688, 256], replicated, may hold values from -0.125 to 0.125
- segment_ids: int32 [8192], P('ctx'), may hold values from 0 to 3, never falling along the last dimension, each value on 1 to 6144 neighbouring positions
Outputs:
- stream: bfloat16 [8192, 2688], P('ctx', 'tp')
- context: bfloat16 [8192, 4096], P('ctx', 'tp')
The draws below stay inside these ranges and needn't reach their ends.
Inputs may be any that keep to these rules, and one draw needn't show every extreme that they name: `segment_ids`: document numbers never fall; every one of the 4 documents has 1 to 6144 positions and one has exactly 6144.
All inputs are finite; a program needn't handle non-finite values.
Results may differ from the reference program's by a relative error of at most 0.04.
Values may be sent and summed in bfloat16 or wider, within the bound.
No kernel may reach another device: no remote copies, remote signals or barrier semaphores. Data moves between devices by JAX's collectives and lax.ppermute only.
A program may use at most 64 MiB of HBM per device.

```python
import math
import jax
import jax.numpy as jnp
import numpy as np
from jax import lax

D = 2688
MHEADS = 64
HEADP = 64
STATE = 128
NGROUPS = 8
QHEADS = 32
KVHEADS = 2
HDIM = 128
TOK_DEV = 256
DOCS = 4
INNER = 4096
SEQ = 8192


def draw_decay_log(key, part):
    return jax.random.uniform(key, (MHEADS,), jnp.float32, -9.0, -3.0)


def draw_attn_gain(key, part):
    return jnp.exp(jax.random.uniform(key, (D,), jnp.float32, math.log(1.5), math.log(4.0)))


def spiked(array, key, source, target, shards_of, factor):
    def block_of(position):
        return (jnp.arange(array.shape[position]) // (array.shape[position] // shards_of)).reshape((-1,) + (1,) * (array.ndim - 1 - position))

    first = jax.random.permutation(key, shards_of)[block_of(target)]
    far = (block_of(target) + shards_of // 2) % shards_of
    return jnp.where((block_of(source) == first) | (block_of(source) == far), factor * array, array)


def block_levels(rng, extent, shards, least, top_value):
    level, own = 1.0, jax.random.fold_in(rng, 6)
    for dim, parts in shards:
        steps = jnp.exp(jax.random.uniform(jax.random.fold_in(own, dim), (parts,), jnp.float32, least / len(shards), top_value / len(shards)))
        level = level * jnp.repeat(steps, extent[dim] // parts).reshape([-1 if axis == dim else 1 for axis in range(len(extent))])
    return level


def length_profile(count, total, bound, lean):
    weights = [(1 << 20) // math.isqrt(rank ** lean) + 1 for rank in range(2, count + 1)]
    surplus, counts = total - bound - (count - 1), [1] * (count - 1)
    while surplus > 0:
        candidates = [i for i in range(count - 1) if counts[i] < bound]
        mass, budget = sum([weights[i] for i in candidates]), surplus
        for i in candidates:
            addition = min(bound - counts[i], max(1, budget * weights[i] // mass), surplus)
            counts[i] = counts[i] + addition
            surplus = surplus - addition
    return np.array([bound] + counts)


def uneven(stream_key, number_of, total, most, slope):
    if number_of == 2:
        one = jax.random.randint(stream_key, (), max(1, total - most), min(most, total - 1) + 1)
        return jnp.stack([one, total - one])
    lengths = jnp.asarray(length_profile(number_of, total, most, slope), jnp.int32)
    pairs = (number_of - 1) // 2
    giver, taker = lengths[1:1 + 2 * pairs:2], lengths[2:2 + 2 * pairs:2]
    slack = jnp.minimum(giver - 1, most - taker)
    moved = jax.random.randint(jax.random.fold_in(stream_key, 1), (pairs,), 0, 1 << 20) % (slack + 1)
    lengths = lengths.at[1:1 + 2 * pairs:2].set(giver - moved).at[2:2 + 2 * pairs:2].set(taker + moved)
    return lengths[jax.random.permutation(jax.random.fold_in(stream_key, 2), number_of)]


def bell_draw(rng, shape, width, limit, shards=(), kind=jnp.bfloat16):
    entries = jax.random.normal(rng, shape, jnp.float32) * width
    if len(shards) > 0:
        entries = block_levels(rng, shape, shards, -0.22, 0.18) * entries
    return jnp.clip(entries, min=-limit, max=limit).astype(kind)


def gaussian_with(own_key, dims, spread, limit, cuts, heavy, kind=jnp.bfloat16):
    result = spread * jax.random.normal(own_key, dims, jnp.float32)
    if cuts:
        result = result * block_levels(own_key, dims, cuts, -0.22, 0.18)
    return jnp.clip(spiked(result, jax.random.fold_in(own_key, 3), *heavy), -limit, limit).astype(kind)


def setup_inputs(seed: int = 0) -> dict:
    streams_of = jax.random.split(jax.random.key(seed), 16)
    hidden = bell_draw(streams_of[0], (SEQ, D), 1.0, 6.0, ((0, 32), (1, 8)))
    mamba_x = bell_draw(streams_of[1], (SEQ, INNER), 1.0, 6.0, ((0, 32), (1, 8)))
    gate_z = bell_draw(streams_of[2], (SEQ, INNER), 1.0, 6.0, ((0, 32), (1, 8)))
    b_input = bell_draw(streams_of[3], (SEQ, NGROUPS * STATE), 1.0, 6.0, ((0, 32), (1, 8)))
    c_input = bell_draw(streams_of[4], (SEQ, NGROUPS * STATE), 0.1, 0.59765625, ((0, 32), (1, 8)))
    dt_raw = bell_draw(streams_of[5], (SEQ, MHEADS), 1.0, 5.0, ((0, 32), (1, 8)), jnp.float32)
    dt_bias = jnp.clip(-2.0 + 3.0 * jax.random.uniform(streams_of[6], (MHEADS,), jnp.float32) ** block_levels(streams_of[6], (MHEADS,), ((0, 8),), -0.2, 0.2), -2.0, 1.0)
    decay_log = draw_decay_log(jax.random.fold_in(streams_of[15], 71), 0)
    d_skip = jnp.clip(0.5 + 1.0 * jax.random.uniform(streams_of[8], (MHEADS,), jnp.float32) ** block_levels(streams_of[8], (MHEADS,), ((0, 8),), -0.2, 0.2), 0.5, 1.5)
    mixer_gain = jnp.clip(1.0 + 0.18 * jax.random.normal(streams_of[9], (INNER,), jnp.float32), 0.1, 1.9)
    out_weight = gaussian_with(streams_of[10], (INNER, D), INNER ** -0.5, 0.125, ((0, 8),), (0, 1, 8, 2.0))
    attn_gain = draw_attn_gain(jax.random.fold_in(streams_of[15], 71), 0)
    w_query = bell_draw(streams_of[12], (D, QHEADS * HDIM), D ** -0.5, 0.125, ((1, 8),))
    w_keyval = bell_draw(streams_of[13], (KVHEADS, D, 2 * HDIM), D ** -0.5, 0.125)
    segment_ids = jnp.searchsorted(jnp.cumsum(uneven(streams_of[14], DOCS, SEQ, 3 * SEQ // 4, 0)), jnp.arange(SEQ), side="right").astype(jnp.int32)
    return {"hidden": hidden, "mamba_x": mamba_x, "gate_z": gate_z, "b_input": b_input, "c_input": c_input, "dt_raw": dt_raw, "dt_bias": dt_bias, "decay_log": decay_log, "d_skip": d_skip, "mixer_gain": mixer_gain, "out_weight": out_weight, "attn_gain": attn_gain, "w_query": w_query, "w_keyval": w_keyval, "segment_ids": segment_ids}


def reference(hidden, mamba_x, gate_z, b_input, c_input, dt_raw, dt_bias, decay_log, d_skip, mixer_gain, out_weight, attn_gain, w_query, w_keyval, segment_ids):
    highest = lax.Precision.HIGHEST
    group_heads = MHEADS // NGROUPS
    blocks = SEQ // TOK_DEV
    segment_prev = jnp.concatenate([jnp.full((1,), -1, jnp.int32), segment_ids[:-1]])
    step_size = jax.nn.softplus(dt_raw + dt_bias[None, :])
    log_decay = -step_size * jnp.exp(decay_log)[None, :]
    inputs_x = mamba_x.astype(jnp.float32).reshape(blocks, TOK_DEV, MHEADS, HEADP)
    inputs_b = b_input.astype(jnp.float32).reshape(blocks, TOK_DEV, NGROUPS, STATE)
    inputs_c = c_input.astype(jnp.float32).reshape(blocks, TOK_DEV, NGROUPS, STATE)
    order = jnp.arange(TOK_DEV, dtype=jnp.int32)
    lower = order[:, None] >= order[None, :]

    def block_step(state, inputs):
        block_x, block_b, block_c, block_log, block_step_size, block_seg, block_prev = inputs
        cumulative = jnp.cumsum(block_log, axis=0)
        cum_heads = cumulative.T
        same = lower & (block_seg[:, None] == block_seg[None, :])
        differ = jnp.where(same[None], cum_heads[:, :, None] - cum_heads[:, None, :], 0.0)
        decay_ts = jnp.where(same[None], jnp.exp(differ), 0.0) * block_step_size.T[:, None, :]
        inner = jnp.einsum('tgn,sgn->gts', block_c, block_b, precision=highest)
        inner = jnp.repeat(inner, group_heads, axis=0)
        local_out = jnp.einsum('hts,shp->thp', inner * decay_ts, block_x, precision=highest)
        keep = (block_seg == block_prev[0]).astype(jnp.float32)
        carry_gain = jnp.exp(cumulative) * keep[:, None]
        c_heads = jnp.repeat(block_c, group_heads, axis=1)
        carry_out = jnp.einsum('thn,hpn->thp', c_heads, state, precision=highest) * carry_gain[:, :, None]
        tail = jnp.exp(cumulative[-1][None, :] - cumulative) * (block_seg == block_seg[-1]).astype(jnp.float32)[:, None] * block_step_size
        b_heads = jnp.repeat(block_b, group_heads, axis=1)
        fresh = jnp.einsum('shp,shn->hpn', block_x * tail[:, :, None], b_heads, precision=highest)
        new_state = carry_gain[-1][:, None, None] * state + fresh
        return (new_state, local_out + carry_out + d_skip[None, :, None] * block_x)
    start_state = jnp.zeros((MHEADS, HEADP, STATE), jnp.float32)
    scanned = (inputs_x, inputs_b, inputs_c, log_decay.reshape(blocks, TOK_DEV, MHEADS), step_size.reshape(blocks, TOK_DEV, MHEADS), segment_ids.reshape(blocks, TOK_DEV), segment_prev.reshape(blocks, TOK_DEV))
    _, outputs = lax.scan(block_step, start_state, scanned)
    ssm_out = outputs.reshape(SEQ, INNER)
    gated = ssm_out * jax.nn.silu(gate_z.astype(jnp.float32))
    grouped = gated.reshape(SEQ, NGROUPS, INNER // NGROUPS)
    inv_rms = lax.rsqrt(lax.optimization_barrier(jnp.mean(grouped * grouped, axis=2, keepdims=True)) + 1e-05)
    mixed = ((grouped * inv_rms).reshape(SEQ, INNER) * mixer_gain[None, :]).astype(jnp.bfloat16)
    stream = (hidden.astype(jnp.float32) + jnp.dot(mixed, out_weight, preferred_element_type=jnp.float32)).astype(jnp.bfloat16)
    stream_f = stream.astype(jnp.float32)
    row_rms = lax.rsqrt(lax.optimization_barrier(jnp.mean(stream_f * stream_f, axis=1, keepdims=True)) + 1e-05)
    normed = (stream_f * row_rms * attn_gain[None, :]).astype(jnp.bfloat16)
    queries = jnp.dot(normed, w_query, preferred_element_type=jnp.float32).astype(jnp.bfloat16)
    keyvals = jnp.stack([jnp.dot(normed, w_keyval[group], preferred_element_type=jnp.float32) for group in range(KVHEADS)]).astype(jnp.bfloat16)
    query_heads = queries.reshape(SEQ, QHEADS, HDIM).transpose(1, 0, 2)
    owners = jnp.arange(QHEADS, dtype=jnp.int32) // (QHEADS // KVHEADS)
    positions = jnp.arange(SEQ, dtype=jnp.int32)
    allowed = (positions[None, :] <= positions[:, None]) & (segment_ids[None, :] == segment_ids[:, None])
    scale = HDIM ** (-0.5)

    def one_head(inputs):
        query_head, owner = inputs
        pair = keyvals[owner]
        keys = pair[:, :HDIM]
        values = pair[:, HDIM:]
        scores = jnp.dot(query_head, keys.T, preferred_element_type=jnp.float32) * scale
        masked = jnp.where(allowed, scores, -1e+30)
        highest_score = lax.optimization_barrier(jnp.max(masked, axis=1, keepdims=True))
        weights = jnp.where(allowed, jnp.exp(scores - highest_score), 0.0)
        total = lax.optimization_barrier(jnp.sum(weights, axis=1, keepdims=True))
        return jnp.dot(weights.astype(jnp.bfloat16), values, preferred_element_type=jnp.float32) / total
    heads_out = lax.map(one_head, (query_heads, owners))
    context = heads_out.transpose(1, 0, 2).reshape(SEQ, QHEADS * HDIM).astype(jnp.bfloat16)
    return (stream, context)
```

```python
import math

import jax
import jax.numpy as jnp
from jax import lax
from jax.experimental import pallas as pl
from jax.experimental.pallas import tpu as pltpu
from jax.sharding import PartitionSpec as P

D = 2688
MHEADS = 64
HEADP = 64
STATE = 128
NGROUPS = 8
QHEADS = 32
KVHEADS = 2
HDIM = 128
MAXDOC = 6144


def combine(earlier, later):
    decay_e, state_e, first_e, last_e = earlier
    decay_l, state_l, first_l, last_l = later
    joined = (last_e == first_l).astype(jnp.float32)
    gain = decay_l * joined
    return (decay_e * gain, gain[:, None, None] * state_e + state_l, first_e, last_l)


def pack(element):
    decay, state, first, last = element
    heads, width, size = state.shape
    meta = jnp.zeros((8, size), jnp.float32)
    meta = meta.at[0, :heads].set(decay)
    meta = meta.at[1, :].set(first)
    meta = meta.at[2, :].set(last)
    return jnp.concatenate([state.reshape(heads * width, size), meta], axis=0)


def unpack(packed, heads, width):
    size = packed.shape[1]
    state = packed[: heads * width].reshape(heads, width, size)
    meta = packed[heads * width :]
    return (meta[0, :heads], state, meta[1, 0], meta[2, 0])


def exclusive_scan(element, axis):
    peers = lax.axis_size(axis)
    position = lax.axis_index(axis)
    heads, width, _ = element[1].shape
    inclusive = element
    before = None
    dist = 1
    while dist < peers:
        pairs = [(j, j + dist) for j in range(peers - dist)]
        got = unpack(lax.ppermute(pack(inclusive), axis, pairs), heads, width)
        reached = position >= dist
        merged = combine(got, inclusive)
        if before is None:
            before = got
        else:
            before = jax.tree.map(
                lambda a, b: jnp.where(reached, a, b), combine(got, before), before
            )
        if dist * 2 < peers:
            inclusive = jax.tree.map(lambda a, b: jnp.where(reached, a, b), merged, inclusive)
        dist *= 2
    return before


def mixer_partial(
    mamba_x, gate_z, b_input, c_input, dt_raw, dt_bias, decay_log, d_skip, mixer_gain, out_weight,
    segment,
):
    highest = lax.Precision.HIGHEST
    rows = mamba_x.shape[0]
    local_heads = dt_raw.shape[1]
    group_heads = MHEADS // NGROUPS
    local_groups = local_heads // group_heads
    position = lax.axis_index("ctx")
    segf = segment.astype(jnp.float32)
    step_size = jax.nn.softplus(dt_raw + dt_bias[None, :])
    cumulative = jnp.cumsum(-step_size * jnp.exp(decay_log)[None, :], axis=0)
    cum_heads = cumulative.T
    order = jnp.arange(rows, dtype=jnp.int32)
    same = (order[:, None] >= order[None, :]) & (segment[:, None] == segment[None, :])
    differ = jnp.where(same[None], cum_heads[:, :, None] - cum_heads[:, None, :], 0.0)
    decay_ts = jnp.where(same[None], jnp.exp(differ), 0.0) * step_size.T[:, None, :]
    heads_x = mamba_x.astype(jnp.float32).reshape(rows, local_heads, HEADP)
    groups_b = b_input.astype(jnp.float32).reshape(rows, local_groups, STATE)
    groups_c = c_input.astype(jnp.float32).reshape(rows, local_groups, STATE)
    tail = (
        jnp.exp(cumulative[-1][None, :] - cumulative)
        * (segment == segment[-1]).astype(jnp.float32)[:, None]
        * step_size
    )
    b_heads = jnp.repeat(groups_b, group_heads, axis=1)
    fresh = jnp.einsum("shp,shn->hpn", heads_x * tail[:, :, None], b_heads, precision=highest)
    whole = (segment[0] == segment[-1]).astype(jnp.float32)
    device_decay = jnp.exp(cumulative[-1]) * whole
    carried_decay, carried, _, last_before = exclusive_scan(
        (device_decay, fresh, segf[0], segf[-1]), "ctx"
    )
    del carried_decay
    inner = jnp.einsum("tgn,sgn->gts", groups_c, groups_b, precision=highest)
    inner = jnp.repeat(inner, group_heads, axis=0)
    local_out = jnp.einsum("hts,shp->thp", inner * decay_ts, heads_x, precision=highest)
    keep = ((segf == last_before) & (position > 0)).astype(jnp.float32)
    carry_gain = jnp.exp(cumulative) * keep[:, None]
    c_heads = jnp.repeat(groups_c, group_heads, axis=1)
    carry_out = (
        jnp.einsum("thn,hpn->thp", c_heads, carried, precision=highest) * carry_gain[:, :, None]
    )
    ssm_out = local_out + carry_out + d_skip[None, :, None] * heads_x
    gated = ssm_out.reshape(rows, local_heads * HEADP) * jax.nn.silu(gate_z.astype(jnp.float32))
    grouped = gated.reshape(rows, local_groups, group_heads * HEADP)
    inv_rms = lax.rsqrt(jnp.mean(grouped * grouped, axis=2, keepdims=True) + 1e-05)
    mixed = ((grouped * inv_rms).reshape(rows, local_heads * HEADP) * mixer_gain[None, :]).astype(
        jnp.bfloat16
    )
    return jnp.dot(mixed, out_weight, preferred_element_type=jnp.float32)


def flash_kernel(where_ref, q_ref, qseg_ref, qpos_ref, kv_ref, o_ref, top_sc, total_sc, acc_sc,
                 q_sc, *, window, rows, heads, width, scale):
    b = pl.program_id(0)
    block = where_ref[0] - (window - 1) + b

    @pl.when(b == 0)
    def _():
        top_sc[...] = jnp.full(top_sc.shape, -1e30, jnp.float32)
        total_sc[...] = jnp.zeros(total_sc.shape, jnp.float32)
        acc_sc[...] = jnp.zeros(acc_sc.shape, jnp.float32)
        for h in range(heads):
            q_sc[h * rows : (h + 1) * rows, :] = q_ref[:, h * width : (h + 1) * width]

    @pl.when(block >= 0)
    def _():
        q = q_sc[...]
        k = kv_ref[0, :rows, :width]
        v = kv_ref[0, :rows, width:]
        kseg = kv_ref[0, rows : rows + 1, :rows].astype(jnp.float32)
        kpos = block * rows + lax.broadcasted_iota(jnp.int32, (1, rows), 1)
        s = lax.dot_general(q, k, (((1,), (1,)), ((), ())), preferred_element_type=jnp.float32)
        s = s * scale
        allowed = (kpos <= qpos_ref[...]) & (kseg == qseg_ref[...])
        masked = jnp.where(allowed, s, -1e30)
        top = top_sc[...]
        new_top = jnp.maximum(top, jnp.max(masked, axis=1, keepdims=True))
        p = jnp.where(allowed, jnp.exp(s - new_top), 0.0)
        factor = jnp.exp(top - new_top)
        total_sc[...] = total_sc[...] * factor + jnp.sum(p, axis=1, keepdims=True)
        acc_sc[...] = acc_sc[...] * factor + jnp.dot(
            p.astype(jnp.bfloat16), v, preferred_element_type=jnp.float32
        )
        top_sc[...] = new_top

    @pl.when(b == window - 1)
    def _():
        out = acc_sc[...] / total_sc[...]
        for h in range(heads):
            o_ref[:, h * width : (h + 1) * width] = out[h * rows : (h + 1) * rows].astype(
                o_ref.dtype
            )


def flash(where, queries, qseg, qpos, blocks, heads):
    window, block_rows, pair = blocks.shape
    rows = queries.shape[0]
    width = pair // 2
    kernel = lambda *refs: flash_kernel(
        *refs, window=window, rows=rows, heads=heads, width=width, scale=width ** (-0.5)
    )

    def kv_map(b, where_ref):
        return (jnp.maximum(b, (window - 1) - where_ref[0]), 0, 0)

    grid_spec = pltpu.PrefetchScalarGridSpec(
        num_scalar_prefetch=1,
        grid=(window,),
        in_specs=[
            pl.BlockSpec((rows, heads * width), lambda b, w: (0, 0)),
            pl.BlockSpec((heads * rows, 1), lambda b, w: (0, 0)),
            pl.BlockSpec((heads * rows, 1), lambda b, w: (0, 0)),
            pl.BlockSpec((1, block_rows, pair), kv_map),
        ],
        out_specs=pl.BlockSpec((rows, heads * width), lambda b, w: (0, 0)),
        scratch_shapes=[
            pltpu.VMEM((heads * rows, 1), jnp.float32),
            pltpu.VMEM((heads * rows, 1), jnp.float32),
            pltpu.VMEM((heads * rows, width), jnp.float32),
            pltpu.VMEM((heads * rows, width), jnp.bfloat16),
        ],
    )
    return pl.pallas_call(
        kernel,
        grid_spec=grid_spec,
        out_shape=jax.ShapeDtypeStruct((rows, heads * width), jnp.bfloat16),
        compiler_params=pltpu.CompilerParams(dimension_semantics=("arbitrary",)),
    )(where, queries, qseg, qpos, blocks)


def body(
    hidden, mamba_x, gate_z, b_input, c_input, dt_raw, dt_bias, decay_log, d_skip, mixer_gain,
    out_weight, attn_gain, w_query, w_keyval, segment_ids,
):
    rows, columns = hidden.shape
    peers = lax.axis_size("ctx")
    position = lax.axis_index("ctx")
    partial_out = mixer_partial(
        mamba_x, gate_z, b_input, c_input, dt_raw, dt_bias, decay_log, d_skip, mixer_gain,
        out_weight, segment_ids,
    )
    tp_index = lax.axis_index("tp")
    local_query = w_query.shape[1] // HDIM
    owner = tp_index * local_query // (QHEADS // KVHEADS)
    w_pair = lax.dynamic_index_in_dim(w_keyval, owner, 0, keepdims=False)
    own_sum = lax.psum_scatter(partial_out, "tp", scatter_dimension=1, tiled=True)
    stream = (hidden.astype(jnp.float32) + own_sum).astype(jnp.bfloat16)
    full = lax.all_gather(stream, "tp", axis=1, tiled=True).astype(jnp.float32)
    inv_rms = lax.rsqrt(jnp.sum(full * full, axis=1) / D + 1e-05)
    normed = (full * inv_rms[:, None] * attn_gain[None, :]).astype(jnp.bfloat16)
    queries = jnp.dot(normed, w_query, preferred_element_type=jnp.float32).astype(jnp.bfloat16)
    pairs = jnp.dot(normed, w_pair, preferred_element_type=jnp.float32).astype(jnp.bfloat16)
    pair_width = pairs.shape[1]
    seg_rows = jnp.zeros((16, pair_width), jnp.bfloat16)
    seg_rows = seg_rows.at[0, :rows].set(segment_ids.astype(jnp.bfloat16))
    own_block = jnp.concatenate([pairs, seg_rows], axis=0)
    back = min(peers - 1, -(-(MAXDOC - 1) // rows))
    received = []
    for dist in range(back, 0, -1):
        pairs_list = [(j, j + dist) for j in range(peers - dist)]
        received.append(lax.ppermute(own_block, "ctx", pairs_list))
    blocks = jnp.stack(received + [own_block], axis=0)
    heads = local_query
    qseg = jnp.tile(segment_ids.astype(jnp.float32), heads)[:, None]
    qpos = jnp.tile(position * rows + jnp.arange(rows, dtype=jnp.int32), heads)[:, None]
    where = jnp.reshape(position, (1,)).astype(jnp.int32)
    context = flash(where, queries, qseg, qpos, blocks, heads)
    return (stream, context)


def solution(mesh):
    in_specs = (
        P("ctx", "tp"),
        P("ctx", "tp"),
        P("ctx", "tp"),
        P("ctx", "tp"),
        P("ctx", "tp"),
        P("ctx", "tp"),
        P("tp"),
        P("tp"),
        P("tp"),
        P("tp"),
        P("tp", None),
        P(),
        P(None, "tp"),
        P(),
        P("ctx"),
    )
    out_specs = (P("ctx", "tp"), P("ctx", "tp"))
    return jax.shard_map(body, mesh=mesh, in_specs=in_specs, out_specs=out_specs, check_vma=False)
```

```python
import math

import jax
import jax.numpy as jnp
from jax import lax
from jax.experimental import pallas as pl
from jax.experimental.pallas import tpu as pltpu
from jax.sharding import PartitionSpec as P

D = 2688
MHEADS = 64
HEADP = 64
STATE = 128
NGROUPS = 8
QHEADS = 32
KVHEADS = 2
HDIM = 128
MAXDOC = 6144


def combine_kernel(flag_ref, got_ref, cur_ref, out_ref, *, heads, width):
    @pl.when(flag_ref[0] > 0)
    def _():
        base = heads * width
        joined = (got_ref[base + 9 : base + 10, :] == cur_ref[base + 8 : base + 9, :]).astype(
            jnp.float32
        )
        for h in range(heads):
            gain = cur_ref[base + h : base + h + 1, :] * joined
            out_ref[h * width : (h + 1) * width, :] = (
                gain * got_ref[h * width : (h + 1) * width, :] + cur_ref[h * width : (h + 1) * width, :]
            )
            out_ref[base + h : base + h + 1, :] = got_ref[base + h : base + h + 1, :] * gain
        out_ref[base + 8 : base + 9, :] = got_ref[base + 8 : base + 9, :]
        out_ref[base + 9 : base + 16, :] = cur_ref[base + 9 : base + 16, :]

    @pl.when(flag_ref[0] == 0)
    def _():
        out_ref[...] = cur_ref[...]


def combine_packed(flag, got, cur, heads, width):
    full = pl.BlockSpec(got.shape, lambda i, f: (0, 0))
    grid_spec = pltpu.PrefetchScalarGridSpec(
        num_scalar_prefetch=1, grid=(1,), in_specs=[full, full], out_specs=full
    )
    kernel = lambda *refs: combine_kernel(*refs, heads=heads, width=width)
    return pl.pallas_call(
        kernel, grid_spec=grid_spec, out_shape=jax.ShapeDtypeStruct(got.shape, got.dtype)
    )(flag, got, cur)


def pack(decay, state, first, last):
    heads, width, size = state.shape
    meta = jnp.concatenate(
        [
            jnp.broadcast_to(decay[:, None], (heads, size)),
            jnp.full((1, size), first, jnp.float32),
            jnp.full((1, size), last, jnp.float32),
            jnp.zeros((6, size), jnp.float32),
        ],
        axis=0,
    )
    return jnp.concatenate([state.reshape(heads * width, size), meta], axis=0)


def exclusive_scan(decay, state, first, last, axis):
    peers = lax.axis_size(axis)
    position = lax.axis_index(axis)
    heads, width, size = state.shape
    assert heads == 8
    inclusive = pack(decay, state, first, last)
    before = None
    dist = 1
    while dist < peers:
        pairs = [(j, j + dist) for j in range(peers - dist)]
        got = lax.ppermute(inclusive, axis, pairs)
        flag = jnp.reshape(position >= dist, (1,)).astype(jnp.int32)
        if before is None:
            before = got
        else:
            before = combine_packed(flag, got, before, heads, width)
        if dist * 2 < peers:
            inclusive = combine_packed(flag, got, inclusive, heads, width)
        dist *= 2
    carried = before[: heads * width].reshape(heads, width, size)
    return carried, before[heads * width + 9, 0]


def mixer_partial(
    mamba_x, gate_z, b_input, c_input, dt_raw, dt_bias, decay_log, d_skip, mixer_gain, out_weight,
    segment,
):
    highest = lax.Precision.HIGHEST
    rows = mamba_x.shape[0]
    local_heads = dt_raw.shape[1]
    group_heads = MHEADS // NGROUPS
    local_groups = local_heads // group_heads
    position = lax.axis_index("ctx")
    segf = segment.astype(jnp.float32)
    step_size = jax.nn.softplus(dt_raw + dt_bias[None, :])
    cumulative = jnp.cumsum(-step_size * jnp.exp(decay_log)[None, :], axis=0)
    cum_heads = cumulative.T
    order = jnp.arange(rows, dtype=jnp.int32)
    same = (order[:, None] >= order[None, :]) & (segment[:, None] == segment[None, :])
    differ = jnp.where(same[None], cum_heads[:, :, None] - cum_heads[:, None, :], 0.0)
    decay_ts = jnp.where(same[None], jnp.exp(differ), 0.0) * step_size.T[:, None, :]
    heads_x = mamba_x.astype(jnp.float32).reshape(rows, local_heads, HEADP)
    groups_b = b_input.astype(jnp.float32).reshape(rows, local_groups, STATE)
    groups_c = c_input.astype(jnp.float32).reshape(rows, local_groups, STATE)
    tail = (
        jnp.exp(cumulative[-1][None, :] - cumulative)
        * (segment == segment[-1]).astype(jnp.float32)[:, None]
        * step_size
    )
    b_heads = jnp.repeat(groups_b, group_heads, axis=1)
    fresh = jnp.einsum("shp,shn->hpn", heads_x * tail[:, :, None], b_heads, precision=highest)
    whole = (segment[0] == segment[-1]).astype(jnp.float32)
    device_decay = jnp.exp(cumulative[-1]) * whole
    carried, last_before = exclusive_scan(device_decay, fresh, segf[0], segf[-1], "ctx")
    inner = jnp.einsum("tgn,sgn->gts", groups_c, groups_b, precision=highest)
    inner = jnp.repeat(inner, group_heads, axis=0)
    local_out = jnp.einsum("hts,shp->thp", inner * decay_ts, heads_x, precision=highest)
    keep = ((segf == last_before) & (position > 0)).astype(jnp.float32)
    carry_gain = jnp.exp(cumulative) * keep[:, None]
    c_heads = jnp.repeat(groups_c, group_heads, axis=1)
    carry_out = (
        jnp.einsum("thn,hpn->thp", c_heads, carried, precision=highest) * carry_gain[:, :, None]
    )
    ssm_out = local_out + carry_out + d_skip[None, :, None] * heads_x
    gated = ssm_out.reshape(rows, local_heads * HEADP) * jax.nn.silu(gate_z.astype(jnp.float32))
    grouped = gated.reshape(rows, local_groups, group_heads * HEADP)
    inv_rms = lax.rsqrt(jnp.mean(grouped * grouped, axis=2, keepdims=True) + 1e-05)
    mixed = ((grouped * inv_rms).reshape(rows, local_heads * HEADP) * mixer_gain[None, :]).astype(
        jnp.bfloat16
    )
    return jnp.dot(mixed, out_weight, preferred_element_type=jnp.float32)


def flash_kernel(where_ref, q_ref, qseg_ref, qpos_ref, kv_ref, o_ref, top_sc, total_sc, acc_sc,
                 q_sc, *, window, rows, heads, width, scale):
    b = pl.program_id(0)
    block = where_ref[0] - (window - 1) + b

    @pl.when(b == 0)
    def _():
        top_sc[...] = jnp.full(top_sc.shape, -1e30, jnp.float32)
        total_sc[...] = jnp.zeros(total_sc.shape, jnp.float32)
        acc_sc[...] = jnp.zeros(acc_sc.shape, jnp.float32)
        for h in range(heads):
            q_sc[h * rows : (h + 1) * rows, :] = q_ref[:, h * width : (h + 1) * width]

    @pl.when(block >= 0)
    def _():
        q = q_sc[...]
        k = kv_ref[0, :rows, :width]
        v = kv_ref[0, :rows, width:]
        kseg = kv_ref[0, rows : rows + 1, :rows].astype(jnp.float32)
        kpos = block * rows + lax.broadcasted_iota(jnp.int32, (1, rows), 1)
        s = lax.dot_general(q, k, (((1,), (1,)), ((), ())), preferred_element_type=jnp.float32)
        s = s * scale
        allowed = (kpos <= qpos_ref[...]) & (kseg == qseg_ref[...])
        masked = jnp.where(allowed, s, -1e30)
        top = top_sc[...]
        new_top = jnp.maximum(top, jnp.max(masked, axis=1, keepdims=True))
        p = jnp.where(allowed, jnp.exp(s - new_top), 0.0)
        factor = jnp.exp(top - new_top)
        total_sc[...] = total_sc[...] * factor + jnp.sum(p, axis=1, keepdims=True)
        acc_sc[...] = acc_sc[...] * factor + jnp.dot(
            p.astype(jnp.bfloat16), v, preferred_element_type=jnp.float32
        )
        top_sc[...] = new_top

    @pl.when(b == window - 1)
    def _():
        out = acc_sc[...] / total_sc[...]
        for h in range(heads):
            o_ref[:, h * width : (h + 1) * width] = out[h * rows : (h + 1) * rows].astype(
                o_ref.dtype
            )


def flash(where, queries, qseg, qpos, blocks, heads):
    window, block_rows, pair = blocks.shape
    rows = queries.shape[0]
    width = pair // 2
    kernel = lambda *refs: flash_kernel(
        *refs, window=window, rows=rows, heads=heads, width=width, scale=width ** (-0.5)
    )

    def kv_map(b, where_ref):
        return (jnp.maximum(b, (window - 1) - where_ref[0]), 0, 0)

    grid_spec = pltpu.PrefetchScalarGridSpec(
        num_scalar_prefetch=1,
        grid=(window,),
        in_specs=[
            pl.BlockSpec((rows, heads * width), lambda b, w: (0, 0)),
            pl.BlockSpec((heads * rows, 1), lambda b, w: (0, 0)),
            pl.BlockSpec((heads * rows, 1), lambda b, w: (0, 0)),
            pl.BlockSpec((1, block_rows, pair), kv_map),
        ],
        out_specs=pl.BlockSpec((rows, heads * width), lambda b, w: (0, 0)),
        scratch_shapes=[
            pltpu.VMEM((heads * rows, 1), jnp.float32),
            pltpu.VMEM((heads * rows, 1), jnp.float32),
            pltpu.VMEM((heads * rows, width), jnp.float32),
            pltpu.VMEM((heads * rows, width), jnp.bfloat16),
        ],
    )
    return pl.pallas_call(
        kernel,
        grid_spec=grid_spec,
        out_shape=jax.ShapeDtypeStruct((rows, heads * width), jnp.bfloat16),
        compiler_params=pltpu.CompilerParams(dimension_semantics=("arbitrary",)),
    )(where, queries, qseg, qpos, blocks)


def body(
    hidden, mamba_x, gate_z, b_input, c_input, dt_raw, dt_bias, decay_log, d_skip, mixer_gain,
    out_weight, attn_gain, w_query, w_keyval, segment_ids,
):
    rows, columns = hidden.shape
    peers = lax.axis_size("ctx")
    position = lax.axis_index("ctx")
    hidden_full = lax.all_gather(hidden, "tp", axis=1, tiled=True)
    partial_out = mixer_partial(
        mamba_x, gate_z, b_input, c_input, dt_raw, dt_bias, decay_log, d_skip, mixer_gain,
        out_weight, segment_ids,
    )
    tp_index = lax.axis_index("tp")
    local_query = w_query.shape[1] // HDIM
    owner = tp_index * local_query // (QHEADS // KVHEADS)
    w_pair = lax.dynamic_index_in_dim(w_keyval, owner, 0, keepdims=False)
    total = lax.psum(partial_out, "tp")
    stream_full = (hidden_full.astype(jnp.float32) + total).astype(jnp.bfloat16)
    stream = lax.dynamic_slice_in_dim(stream_full, tp_index * columns, columns, 1)
    full = stream_full.astype(jnp.float32)
    inv_rms = lax.rsqrt(jnp.sum(full * full, axis=1) / D + 1e-05)
    normed = (full * inv_rms[:, None] * attn_gain[None, :]).astype(jnp.bfloat16)
    queries = jnp.dot(normed, w_query, preferred_element_type=jnp.float32).astype(jnp.bfloat16)
    pairs = jnp.dot(normed, w_pair, preferred_element_type=jnp.float32).astype(jnp.bfloat16)
    pair_width = pairs.shape[1]
    seg_rows = jnp.zeros((16, pair_width), jnp.bfloat16)
    seg_rows = seg_rows.at[0, :rows].set(segment_ids.astype(jnp.bfloat16))
    own_block = jnp.concatenate([pairs, seg_rows], axis=0)
    back = min(peers - 1, -(-(MAXDOC - 1) // rows))
    received = []
    for dist in range(back, 0, -1):
        pairs_list = [(j, j + dist) for j in range(peers - dist)]
        received.append(lax.ppermute(own_block, "ctx", pairs_list))
    blocks = jnp.stack(received + [own_block], axis=0)
    heads = local_query
    qseg = jnp.tile(segment_ids.astype(jnp.float32), heads)[:, None]
    qpos = jnp.tile(position * rows + jnp.arange(rows, dtype=jnp.int32), heads)[:, None]
    where = jnp.reshape(position, (1,)).astype(jnp.int32)
    context = flash(where, queries, qseg, qpos, blocks, heads)
    return (stream, context)


def solution(mesh):
    in_specs = (
        P("ctx", "tp"),
        P("ctx", "tp"),
        P("ctx", "tp"),
        P("ctx", "tp"),
        P("ctx", "tp"),
        P("ctx", "tp"),
        P("tp"),
        P("tp"),
        P("tp"),
        P("tp"),
        P("tp", None),
        P(),
        P(None, "tp"),
        P(),
        P("ctx"),
    )
    out_specs = (P("ctx", "tp"), P("ctx", "tp"))
    return jax.shard_map(body, mesh=mesh, in_specs=in_specs, out_specs=out_specs, check_vma=False)
```

```python
import math

import jax
import jax.numpy as jnp
from jax import lax
from jax.experimental import pallas as pl
from jax.experimental.pallas import tpu as pltpu
from jax.sharding import PartitionSpec as P

D = 2688
MHEADS = 64
HEADP = 64
STATE = 128
NGROUPS = 8
QHEADS = 32
KVHEADS = 2
HDIM = 128
MAXDOC = 6144


def combine_kernel(flag_ref, got_ref, cur_ref, out_ref, *, heads, width):
    @pl.when(flag_ref[0] > 0)
    def _():
        base = heads * width
        joined = (got_ref[base + 9 : base + 10, :] == cur_ref[base + 8 : base + 9, :]).astype(
            jnp.float32
        )
        for h in range(heads):
            gain = cur_ref[base + h : base + h + 1, :] * joined
            out_ref[h * width : (h + 1) * width, :] = (
                gain * got_ref[h * width : (h + 1) * width, :] + cur_ref[h * width : (h + 1) * width, :]
            )
            out_ref[base + h : base + h + 1, :] = got_ref[base + h : base + h + 1, :] * gain
        out_ref[base + 8 : base + 9, :] = got_ref[base + 8 : base + 9, :]
        out_ref[base + 9 : base + 16, :] = cur_ref[base + 9 : base + 16, :]

    @pl.when(flag_ref[0] == 0)
    def _():
        out_ref[...] = cur_ref[...]


def combine_packed(flag, got, cur, heads, width):
    full = pl.BlockSpec(got.shape, lambda i, f: (0, 0))
    grid_spec = pltpu.PrefetchScalarGridSpec(
        num_scalar_prefetch=1, grid=(1,), in_specs=[full, full], out_specs=full
    )
    kernel = lambda *refs: combine_kernel(*refs, heads=heads, width=width)
    return pl.pallas_call(
        kernel, grid_spec=grid_spec, out_shape=jax.ShapeDtypeStruct(got.shape, got.dtype)
    )(flag, got, cur)


def pack(decay, state, first, last):
    heads, width, size = state.shape
    meta = jnp.concatenate(
        [
            jnp.broadcast_to(decay[:, None], (heads, size)),
            jnp.full((1, size), first, jnp.float32),
            jnp.full((1, size), last, jnp.float32),
            jnp.zeros((6, size), jnp.float32),
        ],
        axis=0,
    )
    return jnp.concatenate([state.reshape(heads * width, size), meta], axis=0)


def exclusive_scan(decay, state, first, last, axis):
    peers = lax.axis_size(axis)
    position = lax.axis_index(axis)
    heads, width, size = state.shape
    assert heads == 8
    inclusive = pack(decay, state, first, last)
    before = None
    dist = 1
    while dist < peers:
        pairs = [(j, j + dist) for j in range(peers - dist)]
        got = lax.ppermute(inclusive, axis, pairs)
        flag = jnp.reshape(position >= dist, (1,)).astype(jnp.int32)
        if before is None:
            before = got
        else:
            before = combine_packed(flag, got, before, heads, width)
        if dist * 2 < peers:
            inclusive = combine_packed(flag, got, inclusive, heads, width)
        dist *= 2
    carried = before[: heads * width].reshape(heads, width, size)
    return carried, before[heads * width + 9, 0]


def mixer_partial(
    mamba_x, gate_z, b_input, c_input, dt_raw, dt_bias, decay_log, d_skip, mixer_gain, out_weight,
    segment,
):
    highest = lax.Precision.HIGHEST
    rows = mamba_x.shape[0]
    local_heads = dt_raw.shape[1]
    group_heads = MHEADS // NGROUPS
    local_groups = local_heads // group_heads
    position = lax.axis_index("ctx")
    segf = segment.astype(jnp.float32)
    step_size = jax.nn.softplus(dt_raw + dt_bias[None, :])
    cumulative = jnp.cumsum(-step_size * jnp.exp(decay_log)[None, :], axis=0)
    cum_heads = cumulative.T
    order = jnp.arange(rows, dtype=jnp.int32)
    same = (order[:, None] >= order[None, :]) & (segment[:, None] == segment[None, :])
    differ = jnp.where(same[None], cum_heads[:, :, None] - cum_heads[:, None, :], 0.0)
    decay_ts = jnp.where(same[None], jnp.exp(differ), 0.0) * step_size.T[:, None, :]
    heads_x = mamba_x.astype(jnp.float32).reshape(rows, local_heads, HEADP)
    groups_b = b_input.astype(jnp.float32).reshape(rows, local_groups, STATE)
    groups_c = c_input.astype(jnp.float32).reshape(rows, local_groups, STATE)
    tail = (
        jnp.exp(cumulative[-1][None, :] - cumulative)
        * (segment == segment[-1]).astype(jnp.float32)[:, None]
        * step_size
    )
    b_heads = jnp.repeat(groups_b, group_heads, axis=1)
    fresh = jnp.einsum("shp,shn->hpn", heads_x * tail[:, :, None], b_heads, precision=highest)
    whole = (segment[0] == segment[-1]).astype(jnp.float32)
    device_decay = jnp.exp(cumulative[-1]) * whole
    carried, last_before = exclusive_scan(device_decay, fresh, segf[0], segf[-1], "ctx")
    inner = jnp.einsum("tgn,sgn->gts", groups_c, groups_b, precision=highest)
    inner = jnp.repeat(inner, group_heads, axis=0)
    local_out = jnp.einsum("hts,shp->thp", inner * decay_ts, heads_x, precision=highest)
    keep = ((segf == last_before) & (position > 0)).astype(jnp.float32)
    carry_gain = jnp.exp(cumulative) * keep[:, None]
    c_heads = jnp.repeat(groups_c, group_heads, axis=1)
    carry_out = (
        jnp.einsum("thn,hpn->thp", c_heads, carried, precision=highest) * carry_gain[:, :, None]
    )
    ssm_out = local_out + carry_out + d_skip[None, :, None] * heads_x
    gated = ssm_out.reshape(rows, local_heads * HEADP) * jax.nn.silu(gate_z.astype(jnp.float32))
    grouped = gated.reshape(rows, local_groups, group_heads * HEADP)
    inv_rms = lax.rsqrt(jnp.mean(grouped * grouped, axis=2, keepdims=True) + 1e-05)
    mixed = ((grouped * inv_rms).reshape(rows, local_heads * HEADP) * mixer_gain[None, :]).astype(
        jnp.bfloat16
    )
    return jnp.dot(mixed, out_weight, preferred_element_type=jnp.float32)


def flash_kernel(where_ref, q_ref, qseg_ref, qpos_ref, *rest, window, rows, heads, width, scale):
    kv_refs = rest[:window]
    o_ref, kv_sc, sems, top_sc, total_sc, acc_sc, q_sc = rest[window:]
    first = jnp.maximum(0, (window - 1) - where_ref[0])
    copies = [pltpu.make_async_copy(kv_refs[b], kv_sc.at[b], sems.at[b]) for b in range(window)]
    for b in range(window):
        @pl.when(b >= first)
        def _():
            copies[b].start()

    top_sc[...] = jnp.full(top_sc.shape, -1e30, jnp.float32)
    total_sc[...] = jnp.zeros(total_sc.shape, jnp.float32)
    acc_sc[...] = jnp.zeros(acc_sc.shape, jnp.float32)
    for h in range(heads):
        q_sc[h * rows : (h + 1) * rows, :] = q_ref[:, h * width : (h + 1) * width]
    for b in range(window):
        @pl.when(b >= first)
        def _():
            copies[b].wait()

    def visit(b, carry):
        block = where_ref[0] - (window - 1) + b
        q = q_sc[...]
        k = kv_sc[b, :rows, :width]
        v = kv_sc[b, :rows, width:]
        kseg = kv_sc[b, rows : rows + 1, :rows].astype(jnp.float32)
        kpos = block * rows + lax.broadcasted_iota(jnp.int32, (1, rows), 1)
        s = lax.dot_general(q, k, (((1,), (1,)), ((), ())), preferred_element_type=jnp.float32)
        s = s * scale
        allowed = (kpos <= qpos_ref[...]) & (kseg == qseg_ref[...])
        masked = jnp.where(allowed, s, -1e30)
        top = top_sc[...]
        new_top = jnp.maximum(top, jnp.max(masked, axis=1, keepdims=True))
        p = jnp.where(allowed, jnp.exp(s - new_top), 0.0)
        factor = jnp.exp(top - new_top)
        total_sc[...] = total_sc[...] * factor + jnp.sum(p, axis=1, keepdims=True)
        acc_sc[...] = acc_sc[...] * factor + jnp.dot(
            p.astype(jnp.bfloat16), v, preferred_element_type=jnp.float32
        )
        top_sc[...] = new_top
        return carry

    lax.fori_loop(first, window, visit, 0)
    out = acc_sc[...] / total_sc[...]
    for h in range(heads):
        o_ref[:, h * width : (h + 1) * width] = out[h * rows : (h + 1) * rows].astype(o_ref.dtype)


def flash(where, queries, qseg, qpos, blocks, heads):
    window = len(blocks)
    rows = queries.shape[0]
    block_rows, pair = blocks[0].shape
    width = pair // 2
    kernel = lambda *refs: flash_kernel(
        *refs, window=window, rows=rows, heads=heads, width=width, scale=width ** (-0.5)
    )
    vmem = pltpu.MemorySpace.VMEM
    smem = pltpu.MemorySpace.SMEM
    return pl.pallas_call(
        kernel,
        in_specs=[pl.BlockSpec(memory_space=smem)]
        + [pl.BlockSpec(memory_space=vmem)] * 3
        + [pl.BlockSpec(memory_space=pl.ANY)] * window,
        out_specs=pl.BlockSpec(memory_space=vmem),
        out_shape=jax.ShapeDtypeStruct((rows, heads * width), jnp.bfloat16),
        scratch_shapes=[
            pltpu.VMEM((window, block_rows, pair), jnp.bfloat16),
            pltpu.SemaphoreType.DMA((window,)),
            pltpu.VMEM((heads * rows, 1), jnp.float32),
            pltpu.VMEM((heads * rows, 1), jnp.float32),
            pltpu.VMEM((heads * rows, width), jnp.float32),
            pltpu.VMEM((heads * rows, width), jnp.bfloat16),
        ],
    )(where, queries, qseg, qpos, *blocks)


def body(
    hidden, mamba_x, gate_z, b_input, c_input, dt_raw, dt_bias, decay_log, d_skip, mixer_gain,
    out_weight, attn_gain, w_query, w_keyval, segment_ids,
):
    rows, columns = hidden.shape
    peers = lax.axis_size("ctx")
    position = lax.axis_index("ctx")
    partial_out = mixer_partial(
        mamba_x, gate_z, b_input, c_input, dt_raw, dt_bias, decay_log, d_skip, mixer_gain,
        out_weight, segment_ids,
    )
    tp_index = lax.axis_index("tp")
    local_query = w_query.shape[1] // HDIM
    owner = tp_index * local_query // (QHEADS // KVHEADS)
    w_pair = lax.dynamic_index_in_dim(w_keyval, owner, 0, keepdims=False)
    own_sum = lax.psum_scatter(partial_out, "tp", scatter_dimension=1, tiled=True)
    stream = (hidden.astype(jnp.float32) + own_sum).astype(jnp.bfloat16)
    full = lax.all_gather(stream, "tp", axis=1, tiled=True).astype(jnp.float32)
    inv_rms = lax.rsqrt(jnp.sum(full * full, axis=1) / D + 1e-05)
    normed = (full * inv_rms[:, None] * attn_gain[None, :]).astype(jnp.bfloat16)
    queries = jnp.dot(normed, w_query, preferred_element_type=jnp.float32).astype(jnp.bfloat16)
    pairs = jnp.dot(normed, w_pair, preferred_element_type=jnp.float32).astype(jnp.bfloat16)
    pair_width = pairs.shape[1]
    seg_rows = jnp.zeros((16, pair_width), jnp.bfloat16)
    seg_rows = seg_rows.at[0, :rows].set(segment_ids.astype(jnp.bfloat16))
    own_block = jnp.concatenate([pairs, seg_rows], axis=0)
    back = min(peers - 1, -(-(MAXDOC - 1) // rows))
    received = []
    for dist in range(back, 0, -1):
        pairs_list = [(j, j + dist) for j in range(peers - dist)]
        received.append(lax.ppermute(own_block, "ctx", pairs_list))
    blocks = received + [own_block]
    heads = local_query
    qseg = jnp.tile(segment_ids.astype(jnp.float32), heads)[:, None]
    qpos = jnp.tile(position * rows + jnp.arange(rows, dtype=jnp.int32), heads)[:, None]
    where = jnp.reshape(position, (1,)).astype(jnp.int32)
    context = flash(where, queries, qseg, qpos, blocks, heads)
    return (stream, context)


def solution(mesh):
    in_specs = (
        P("ctx", "tp"),
        P("ctx", "tp"),
        P("ctx", "tp"),
        P("ctx", "tp"),
        P("ctx", "tp"),
        P("ctx", "tp"),
        P("tp"),
        P("tp"),
        P("tp"),
        P("tp"),
        P("tp", None),
        P(),
        P(None, "tp"),
        P(),
        P("ctx"),
    )
    out_specs = (P("ctx", "tp"), P("ctx", "tp"))
    return jax.shard_map(body, mesh=mesh, in_specs=in_specs, out_specs=out_specs, check_vma=False)
```

```python
import math

import jax
import jax.numpy as jnp
from jax import lax
from jax.experimental import pallas as pl
from jax.experimental.pallas import tpu as pltpu
from jax.sharding import PartitionSpec as P

D = 2688
MHEADS = 64
HEADP = 64
STATE = 128
NGROUPS = 8
QHEADS = 32
KVHEADS = 2
HDIM = 128
MAXDOC = 6144


def fold_kernel(flag_ref, *refs, count, outs, heads, width):
    gots = refs[:count]
    curs = refs[count : count + outs]
    results = refs[count + outs :]
    base = heads * width
    for cur_ref, out_ref in zip(curs, results):
        out_ref[...] = cur_ref[...]
        for j, got_ref in enumerate(gots):

            @pl.when(flag_ref[j] > 0)
            def _():
                joined = (
                    got_ref[base + 9 : base + 10, :] == out_ref[base + 8 : base + 9, :]
                ).astype(jnp.float32)
                for h in range(heads):
                    gain = out_ref[base + h : base + h + 1, :] * joined
                    out_ref[h * width : (h + 1) * width, :] = (
                        gain * got_ref[h * width : (h + 1) * width, :]
                        + out_ref[h * width : (h + 1) * width, :]
                    )
                    out_ref[base + h : base + h + 1, :] = got_ref[base + h : base + h + 1, :] * gain
                out_ref[base + 8 : base + 9, :] = got_ref[base + 8 : base + 9, :]


def fold(flags, gots, curs, heads, width):
    vmem = pltpu.MemorySpace.VMEM
    kernel = lambda *refs: fold_kernel(
        *refs, count=len(gots), outs=len(curs), heads=heads, width=width
    )
    return pl.pallas_call(
        kernel,
        in_specs=[pl.BlockSpec(memory_space=pltpu.MemorySpace.SMEM)]
        + [pl.BlockSpec(memory_space=vmem)] * (len(gots) + len(curs)),
        out_specs=[pl.BlockSpec(memory_space=vmem)] * len(curs),
        out_shape=[jax.ShapeDtypeStruct(c.shape, c.dtype) for c in curs],
    )(flags, *gots, *curs)


def pack(decay, state, first, last):
    heads, width, size = state.shape
    meta = jnp.concatenate(
        [
            jnp.broadcast_to(decay[:, None], (heads, size)),
            jnp.full((1, size), first, jnp.float32),
            jnp.full((1, size), last, jnp.float32),
            jnp.zeros((6, size), jnp.float32),
        ],
        axis=0,
    )
    return jnp.concatenate([state.reshape(heads * width, size), meta], axis=0)


def exclusive_scan(decay, state, first, last, axis):
    peers = lax.axis_size(axis)
    position = lax.axis_index(axis)
    heads, width, size = state.shape
    assert heads == 8
    inclusive = pack(decay, state, first, last)
    before = None
    base = 1
    while base < peers:
        dists = [base * k for k in (1, 2, 3) if base * k < peers]
        gots = [
            lax.ppermute(inclusive, axis, [(j, j + d) for j in range(peers - d)]) for d in dists
        ]
        flags = jnp.stack([position >= d for d in dists]).astype(jnp.int32)
        curs = [] if before is None else [before]
        if base * 4 < peers:
            curs.append(inclusive)
        if before is None:
            folded = fold(flags, gots, [inclusive], heads, width) if curs else []
            rest = fold(flags[1:], gots[1:], [gots[0]], heads, width) if len(gots) > 1 else [gots[0]]
            before = rest[0]
            if curs:
                inclusive = folded[0]
        else:
            folded = fold(flags, gots, curs, heads, width)
            before = folded[0]
            if len(folded) > 1:
                inclusive = folded[1]
        base *= 4
    carried = before[: heads * width].reshape(heads, width, size)
    return carried, before[heads * width + 9, 0]


def mixer_partial(
    mamba_x, gate_z, b_input, c_input, dt_raw, dt_bias, decay_log, d_skip, mixer_gain, out_weight,
    segment,
):
    highest = lax.Precision.HIGHEST
    rows = mamba_x.shape[0]
    local_heads = dt_raw.shape[1]
    group_heads = MHEADS // NGROUPS
    local_groups = local_heads // group_heads
    position = lax.axis_index("ctx")
    segf = segment.astype(jnp.float32)
    step_size = jax.nn.softplus(dt_raw + dt_bias[None, :])
    cumulative = jnp.cumsum(-step_size * jnp.exp(decay_log)[None, :], axis=0)
    cum_heads = cumulative.T
    order = jnp.arange(rows, dtype=jnp.int32)
    same = (order[:, None] >= order[None, :]) & (segment[:, None] == segment[None, :])
    differ = jnp.where(same[None], cum_heads[:, :, None] - cum_heads[:, None, :], 0.0)
    decay_ts = jnp.where(same[None], jnp.exp(differ), 0.0) * step_size.T[:, None, :]
    heads_x = mamba_x.astype(jnp.float32).reshape(rows, local_heads, HEADP)
    groups_b = b_input.astype(jnp.float32).reshape(rows, local_groups, STATE)
    groups_c = c_input.astype(jnp.float32).reshape(rows, local_groups, STATE)
    tail = (
        jnp.exp(cumulative[-1][None, :] - cumulative)
        * (segment == segment[-1]).astype(jnp.float32)[:, None]
        * step_size
    )
    b_heads = jnp.repeat(groups_b, group_heads, axis=1)
    fresh = jnp.einsum("shp,shn->hpn", heads_x * tail[:, :, None], b_heads, precision=highest)
    whole = (segment[0] == segment[-1]).astype(jnp.float32)
    device_decay = jnp.exp(cumulative[-1]) * whole
    carried, last_before = exclusive_scan(device_decay, fresh, segf[0], segf[-1], "ctx")
    inner = jnp.einsum("tgn,sgn->gts", groups_c, groups_b, precision=highest)
    inner = jnp.repeat(inner, group_heads, axis=0)
    local_out = jnp.einsum("hts,shp->thp", inner * decay_ts, heads_x, precision=highest)
    keep = ((segf == last_before) & (position > 0)).astype(jnp.float32)
    carry_gain = jnp.exp(cumulative) * keep[:, None]
    c_heads = jnp.repeat(groups_c, group_heads, axis=1)
    carry_out = (
        jnp.einsum("thn,hpn->thp", c_heads, carried, precision=highest) * carry_gain[:, :, None]
    )
    ssm_out = local_out + carry_out + d_skip[None, :, None] * heads_x
    gated = ssm_out.reshape(rows, local_heads * HEADP) * jax.nn.silu(gate_z.astype(jnp.float32))
    grouped = gated.reshape(rows, local_groups, group_heads * HEADP)
    inv_rms = lax.rsqrt(jnp.mean(grouped * grouped, axis=2, keepdims=True) + 1e-05)
    mixed = ((grouped * inv_rms).reshape(rows, local_heads * HEADP) * mixer_gain[None, :]).astype(
        jnp.bfloat16
    )
    return jnp.dot(mixed, out_weight, preferred_element_type=jnp.float32)


def flash_kernel(where_ref, q_ref, qseg_ref, qpos_ref, *rest, window, rows, heads, width, scale):
    kv_refs = rest[:window]
    o_ref, kv_sc, sems, top_sc, total_sc, acc_sc, q_sc = rest[window:]
    own = window - 1
    first = jnp.maximum(0, own - where_ref[0])
    copies = [pltpu.make_async_copy(kv_refs[b], kv_sc.at[b], sems.at[b]) for b in range(window)]
    copies[own].start()
    for b in range(own):

        @pl.when(b >= first)
        def _():
            copies[b].start()

    top_sc[...] = jnp.full(top_sc.shape, -1e30, jnp.float32)
    total_sc[...] = jnp.zeros(total_sc.shape, jnp.float32)
    acc_sc[...] = jnp.zeros(acc_sc.shape, jnp.float32)
    for h in range(heads):
        q_sc[h * rows : (h + 1) * rows, :] = q_ref[:, h * width : (h + 1) * width]

    def update(index, causal):
        q = q_sc[...]
        k = kv_sc[index, :rows, :width]
        v = kv_sc[index, :rows, width:]
        kseg = kv_sc[index, rows : rows + 1, :rows].astype(jnp.float32)
        s = lax.dot_general(q, k, (((1,), (1,)), ((), ())), preferred_element_type=jnp.float32)
        s = s * scale
        allowed = kseg == qseg_ref[...]
        if causal:
            kpos = where_ref[0] * rows + lax.broadcasted_iota(jnp.int32, (1, rows), 1)
            allowed = allowed & (kpos <= qpos_ref[...])
        masked = jnp.where(allowed, s, -1e30)
        top = top_sc[...]
        new_top = jnp.maximum(top, jnp.max(masked, axis=1, keepdims=True))
        p = jnp.exp(masked - new_top)
        factor = jnp.exp(top - new_top)
        total_sc[...] = total_sc[...] * factor + jnp.sum(p, axis=1, keepdims=True)
        acc_sc[...] = acc_sc[...] * factor + jnp.dot(
            p.astype(jnp.bfloat16), v, preferred_element_type=jnp.float32
        )
        top_sc[...] = new_top

    copies[own].wait()
    update(own, True)

    def visit(b, carry):
        for bb in range(own):

            @pl.when(b == bb)
            def _():
                copies[bb].wait()

        update(b, False)
        return carry

    lax.fori_loop(first, own, visit, 0)
    out = acc_sc[...] / total_sc[...]
    for h in range(heads):
        o_ref[:, h * width : (h + 1) * width] = out[h * rows : (h + 1) * rows].astype(o_ref.dtype)


def flash(where, queries, qseg, qpos, blocks, heads):
    window = len(blocks)
    rows = queries.shape[0]
    block_rows, pair = blocks[0].shape
    width = pair // 2
    kernel = lambda *refs: flash_kernel(
        *refs, window=window, rows=rows, heads=heads, width=width, scale=width ** (-0.5)
    )
    vmem = pltpu.MemorySpace.VMEM
    smem = pltpu.MemorySpace.SMEM
    return pl.pallas_call(
        kernel,
        in_specs=[pl.BlockSpec(memory_space=smem)]
        + [pl.BlockSpec(memory_space=vmem)] * 3
        + [pl.BlockSpec(memory_space=pl.ANY)] * window,
        out_specs=pl.BlockSpec(memory_space=vmem),
        out_shape=jax.ShapeDtypeStruct((rows, heads * width), jnp.bfloat16),
        scratch_shapes=[
            pltpu.VMEM((window, block_rows, pair), jnp.bfloat16),
            pltpu.SemaphoreType.DMA((window,)),
            pltpu.VMEM((heads * rows, 1), jnp.float32),
            pltpu.VMEM((heads * rows, 1), jnp.float32),
            pltpu.VMEM((heads * rows, width), jnp.float32),
            pltpu.VMEM((heads * rows, width), jnp.bfloat16),
        ],
    )(where, queries, qseg, qpos, *blocks)


def body(
    hidden, mamba_x, gate_z, b_input, c_input, dt_raw, dt_bias, decay_log, d_skip, mixer_gain,
    out_weight, attn_gain, w_query, w_keyval, segment_ids,
):
    rows, columns = hidden.shape
    peers = lax.axis_size("ctx")
    position = lax.axis_index("ctx")
    partial_out = mixer_partial(
        mamba_x, gate_z, b_input, c_input, dt_raw, dt_bias, decay_log, d_skip, mixer_gain,
        out_weight, segment_ids,
    )
    tp_index = lax.axis_index("tp")
    local_query = w_query.shape[1] // HDIM
    owner = tp_index * local_query // (QHEADS // KVHEADS)
    w_pair = lax.dynamic_index_in_dim(w_keyval, owner, 0, keepdims=False)
    own_sum = lax.psum_scatter(partial_out, "tp", scatter_dimension=1, tiled=True)
    stream = (hidden.astype(jnp.float32) + own_sum).astype(jnp.bfloat16)
    full = lax.all_gather(stream, "tp", axis=1, tiled=True).astype(jnp.float32)
    inv_rms = lax.rsqrt(jnp.sum(full * full, axis=1) / D + 1e-05)
    normed = (full * inv_rms[:, None] * attn_gain[None, :]).astype(jnp.bfloat16)
    queries = jnp.dot(normed, w_query, preferred_element_type=jnp.float32).astype(jnp.bfloat16)
    pairs = jnp.dot(normed, w_pair, preferred_element_type=jnp.float32).astype(jnp.bfloat16)
    pair_width = pairs.shape[1]
    seg_rows = jnp.zeros((16, pair_width), jnp.bfloat16)
    seg_rows = seg_rows.at[0, :rows].set(segment_ids.astype(jnp.bfloat16))
    own_block = jnp.concatenate([pairs, seg_rows], axis=0)
    back = min(peers - 1, -(-(MAXDOC - 1) // rows))
    received = []
    for dist in range(back, 0, -1):
        pairs_list = [(j, j + dist) for j in range(peers - dist)]
        received.append(lax.ppermute(own_block, "ctx", pairs_list))
    blocks = received + [own_block]
    heads = local_query
    qseg = jnp.tile(segment_ids.astype(jnp.float32), heads)[:, None]
    qpos = jnp.tile(position * rows + jnp.arange(rows, dtype=jnp.int32), heads)[:, None]
    where = jnp.reshape(position, (1,)).astype(jnp.int32)
    context = flash(where, queries, qseg, qpos, blocks, heads)
    return (stream, context)


def solution(mesh):
    in_specs = (
        P("ctx", "tp"),
        P("ctx", "tp"),
        P("ctx", "tp"),
        P("ctx", "tp"),
        P("ctx", "tp"),
        P("ctx", "tp"),
        P("tp"),
        P("tp"),
        P("tp"),
        P("tp"),
        P("tp", None),
        P(),
        P(None, "tp"),
        P(),
        P("ctx"),
    )
    out_specs = (P("ctx", "tp"), P("ctx", "tp"))
    return jax.shard_map(body, mesh=mesh, in_specs=in_specs, out_specs=out_specs, check_vma=False)
```

```python
import math

import jax
import jax.numpy as jnp
from jax import lax
from jax.experimental import pallas as pl
from jax.experimental.pallas import tpu as pltpu
from jax.sharding import PartitionSpec as P

D = 2688
MHEADS = 64
HEADP = 64
STATE = 128
NGROUPS = 8
QHEADS = 32
KVHEADS = 2
HDIM = 128
MAXDOC = 6144


def fold_kernel(flag_ref, *refs, count, outs, heads, width):
    gots = refs[:count]
    curs = refs[count : count + outs]
    results = refs[count + outs :]
    base = heads * width
    for cur_ref, out_ref in zip(curs, results):
        out_ref[...] = cur_ref[...]
        for j, got_ref in enumerate(gots):

            @pl.when(flag_ref[j] > 0)
            def _():
                joined = (
                    got_ref[base + 9 : base + 10, :] == out_ref[base + 8 : base + 9, :]
                ).astype(jnp.float32)
                for h in range(heads):
                    gain = out_ref[base + h : base + h + 1, :] * joined
                    out_ref[h * width : (h + 1) * width, :] = (
                        gain * got_ref[h * width : (h + 1) * width, :]
                        + out_ref[h * width : (h + 1) * width, :]
                    )
                    out_ref[base + h : base + h + 1, :] = got_ref[base + h : base + h + 1, :] * gain
                out_ref[base + 8 : base + 9, :] = got_ref[base + 8 : base + 9, :]


def fold(flags, gots, curs, heads, width):
    vmem = pltpu.MemorySpace.VMEM
    kernel = lambda *refs: fold_kernel(
        *refs, count=len(gots), outs=len(curs), heads=heads, width=width
    )
    return pl.pallas_call(
        kernel,
        in_specs=[pl.BlockSpec(memory_space=pltpu.MemorySpace.SMEM)]
        + [pl.BlockSpec(memory_space=vmem)] * (len(gots) + len(curs)),
        out_specs=[pl.BlockSpec(memory_space=vmem)] * len(curs),
        out_shape=[jax.ShapeDtypeStruct(c.shape, c.dtype) for c in curs],
    )(flags, *gots, *curs)


def pack(decay, state, first, last):
    heads, width, size = state.shape
    meta = jnp.concatenate(
        [
            jnp.broadcast_to(decay[:, None], (heads, size)),
            jnp.full((1, size), first, jnp.float32),
            jnp.full((1, size), last, jnp.float32),
            jnp.zeros((6, size), jnp.float32),
        ],
        axis=0,
    )
    return jnp.concatenate([state.reshape(heads * width, size), meta], axis=0)


def exclusive_scan(decay, state, first, last, axis):
    peers = lax.axis_size(axis)
    position = lax.axis_index(axis)
    heads, width, size = state.shape
    assert heads == 8
    inclusive = pack(decay, state, first, last)
    before = None
    dist = 1
    while dist < peers:
        pairs = [(j, j + dist) for j in range(peers - dist)]
        sent = inclusive.astype(jnp.bfloat16)
        got = lax.ppermute(sent, axis, pairs).astype(jnp.float32)
        flags = jnp.reshape(position >= dist, (1,)).astype(jnp.int32)
        curs = [] if before is None else [before]
        if dist * 2 < peers:
            curs.append(inclusive)
        folded = fold(flags, [got], curs, heads, width) if curs else []
        if before is None:
            before = got
            if folded:
                inclusive = folded[0]
        else:
            before = folded[0]
            if len(folded) > 1:
                inclusive = folded[1]
        dist *= 2
    carried = before[: heads * width].reshape(heads, width, size)
    return carried, before[heads * width + 9, 0]


def mixer_partial(
    mamba_x, gate_z, b_input, c_input, dt_raw, dt_bias, decay_log, d_skip, mixer_gain, out_weight,
    segment,
):
    highest = lax.Precision.HIGHEST
    rows = mamba_x.shape[0]
    local_heads = dt_raw.shape[1]
    group_heads = MHEADS // NGROUPS
    local_groups = local_heads // group_heads
    position = lax.axis_index("ctx")
    segf = segment.astype(jnp.float32)
    step_size = jax.nn.softplus(dt_raw + dt_bias[None, :])
    cumulative = jnp.cumsum(-step_size * jnp.exp(decay_log)[None, :], axis=0)
    cum_heads = cumulative.T
    order = jnp.arange(rows, dtype=jnp.int32)
    same = (order[:, None] >= order[None, :]) & (segment[:, None] == segment[None, :])
    differ = jnp.where(same[None], cum_heads[:, :, None] - cum_heads[:, None, :], 0.0)
    decay_ts = jnp.where(same[None], jnp.exp(differ), 0.0) * step_size.T[:, None, :]
    heads_x = mamba_x.astype(jnp.float32).reshape(rows, local_heads, HEADP)
    groups_b = b_input.astype(jnp.float32).reshape(rows, local_groups, STATE)
    groups_c = c_input.astype(jnp.float32).reshape(rows, local_groups, STATE)
    tail = (
        jnp.exp(cumulative[-1][None, :] - cumulative)
        * (segment == segment[-1]).astype(jnp.float32)[:, None]
        * step_size
    )
    b_heads = jnp.repeat(groups_b, group_heads, axis=1)
    fresh = jnp.einsum("shp,shn->hpn", heads_x * tail[:, :, None], b_heads, precision=highest)
    whole = (segment[0] == segment[-1]).astype(jnp.float32)
    device_decay = jnp.exp(cumulative[-1]) * whole
    carried, last_before = exclusive_scan(device_decay, fresh, segf[0], segf[-1], "ctx")
    inner = jnp.einsum("tgn,sgn->gts", groups_c, groups_b, precision=highest)
    inner = jnp.repeat(inner, group_heads, axis=0)
    local_out = jnp.einsum("hts,shp->thp", inner * decay_ts, heads_x, precision=highest)
    keep = ((segf == last_before) & (position > 0)).astype(jnp.float32)
    carry_gain = jnp.exp(cumulative) * keep[:, None]
    c_heads = jnp.repeat(groups_c, group_heads, axis=1)
    carry_out = (
        jnp.einsum("thn,hpn->thp", c_heads, carried, precision=highest) * carry_gain[:, :, None]
    )
    ssm_out = local_out + carry_out + d_skip[None, :, None] * heads_x
    gated = ssm_out.reshape(rows, local_heads * HEADP) * jax.nn.silu(gate_z.astype(jnp.float32))
    grouped = gated.reshape(rows, local_groups, group_heads * HEADP)
    inv_rms = lax.rsqrt(jnp.mean(grouped * grouped, axis=2, keepdims=True) + 1e-05)
    mixed = ((grouped * inv_rms).reshape(rows, local_heads * HEADP) * mixer_gain[None, :]).astype(
        jnp.bfloat16
    )
    return jnp.dot(mixed, out_weight, preferred_element_type=jnp.float32)


def flash_kernel(where_ref, q_ref, qseg_ref, qpos_ref, *rest, window, rows, heads, width, scale):
    kv_refs = rest[:window]
    o_ref, kv_sc, sems, top_sc, total_sc, acc_sc, q_sc = rest[window:]
    first = jnp.maximum(0, (window - 1) - where_ref[0])
    copies = [pltpu.make_async_copy(kv_refs[b], kv_sc.at[b], sems.at[b]) for b in range(window)]
    for b in range(window):
        @pl.when(b >= first)
        def _():
            copies[b].start()

    top_sc[...] = jnp.full(top_sc.shape, -1e30, jnp.float32)
    total_sc[...] = jnp.zeros(total_sc.shape, jnp.float32)
    acc_sc[...] = jnp.zeros(acc_sc.shape, jnp.float32)
    for h in range(heads):
        q_sc[h * rows : (h + 1) * rows, :] = q_ref[:, h * width : (h + 1) * width]
    for b in range(window):
        @pl.when(b >= first)
        def _():
            copies[b].wait()

    def visit(b, carry):
        block = where_ref[0] - (window - 1) + b
        q = q_sc[...]
        k = kv_sc[b, :rows, :width]
        v = kv_sc[b, :rows, width:]
        kseg = kv_sc[b, rows : rows + 1, :rows].astype(jnp.float32)
        kpos = block * rows + lax.broadcasted_iota(jnp.int32, (1, rows), 1)
        s = lax.dot_general(q, k, (((1,), (1,)), ((), ())), preferred_element_type=jnp.float32)
        s = s * scale
        allowed = (kpos <= qpos_ref[...]) & (kseg == qseg_ref[...])
        masked = jnp.where(allowed, s, -1e30)
        top = top_sc[...]
        new_top = jnp.maximum(top, jnp.max(masked, axis=1, keepdims=True))
        p = jnp.where(allowed, jnp.exp(s - new_top), 0.0)
        factor = jnp.exp(top - new_top)
        total_sc[...] = total_sc[...] * factor + jnp.sum(p, axis=1, keepdims=True)
        acc_sc[...] = acc_sc[...] * factor + jnp.dot(
            p.astype(jnp.bfloat16), v, preferred_element_type=jnp.float32
        )
        top_sc[...] = new_top
        return carry

    lax.fori_loop(first, window, visit, 0)
    out = acc_sc[...] / total_sc[...]
    for h in range(heads):
        o_ref[:, h * width : (h + 1) * width] = out[h * rows : (h + 1) * rows].astype(o_ref.dtype)


def flash(where, queries, qseg, qpos, blocks, heads):
    window = len(blocks)
    rows = queries.shape[0]
    block_rows, pair = blocks[0].shape
    width = pair // 2
    kernel = lambda *refs: flash_kernel(
        *refs, window=window, rows=rows, heads=heads, width=width, scale=width ** (-0.5)
    )
    vmem = pltpu.MemorySpace.VMEM
    smem = pltpu.MemorySpace.SMEM
    return pl.pallas_call(
        kernel,
        in_specs=[pl.BlockSpec(memory_space=smem)]
        + [pl.BlockSpec(memory_space=vmem)] * 3
        + [pl.BlockSpec(memory_space=pl.ANY)] * window,
        out_specs=pl.BlockSpec(memory_space=vmem),
        out_shape=jax.ShapeDtypeStruct((rows, heads * width), jnp.bfloat16),
        scratch_shapes=[
            pltpu.VMEM((window, block_rows, pair), jnp.bfloat16),
            pltpu.SemaphoreType.DMA((window,)),
            pltpu.VMEM((heads * rows, 1), jnp.float32),
            pltpu.VMEM((heads * rows, 1), jnp.float32),
            pltpu.VMEM((heads * rows, width), jnp.float32),
            pltpu.VMEM((heads * rows, width), jnp.bfloat16),
        ],
    )(where, queries, qseg, qpos, *blocks)


def body(
    hidden, mamba_x, gate_z, b_input, c_input, dt_raw, dt_bias, decay_log, d_skip, mixer_gain,
    out_weight, attn_gain, w_query, w_keyval, segment_ids,
):
    rows, columns = hidden.shape
    peers = lax.axis_size("ctx")
    position = lax.axis_index("ctx")
    partial_out = mixer_partial(
        mamba_x, gate_z, b_input, c_input, dt_raw, dt_bias, decay_log, d_skip, mixer_gain,
        out_weight, segment_ids,
    )
    tp_index = lax.axis_index("tp")
    local_query = w_query.shape[1] // HDIM
    owner = tp_index * local_query // (QHEADS // KVHEADS)
    w_pair = lax.dynamic_index_in_dim(w_keyval, owner, 0, keepdims=False)
    own_sum = lax.psum_scatter(partial_out, "tp", scatter_dimension=1, tiled=True)
    stream = (hidden.astype(jnp.float32) + own_sum).astype(jnp.bfloat16)
    full = lax.all_gather(stream, "tp", axis=1, tiled=True).astype(jnp.float32)
    inv_rms = lax.rsqrt(jnp.sum(full * full, axis=1) / D + 1e-05)
    normed = (full * inv_rms[:, None] * attn_gain[None, :]).astype(jnp.bfloat16)
    queries = jnp.dot(normed, w_query, preferred_element_type=jnp.float32).astype(jnp.bfloat16)
    pairs = jnp.dot(normed, w_pair, preferred_element_type=jnp.float32).astype(jnp.bfloat16)
    pair_width = pairs.shape[1]
    seg_rows = jnp.zeros((16, pair_width), jnp.bfloat16)
    seg_rows = seg_rows.at[0, :rows].set(segment_ids.astype(jnp.bfloat16))
    own_block = jnp.concatenate([pairs, seg_rows], axis=0)
    back = min(peers - 1, -(-(MAXDOC - 1) // rows))
    received = []
    for dist in range(back, 0, -1):
        pairs_list = [(j, j + dist) for j in range(peers - dist)]
        received.append(lax.ppermute(own_block, "ctx", pairs_list))
    blocks = received + [own_block]
    heads = local_query
    qseg = jnp.tile(segment_ids.astype(jnp.float32), heads)[:, None]
    qpos = jnp.tile(position * rows + jnp.arange(rows, dtype=jnp.int32), heads)[:, None]
    where = jnp.reshape(position, (1,)).astype(jnp.int32)
    context = flash(where, queries, qseg, qpos, blocks, heads)
    return (stream, context)


def solution(mesh):
    in_specs = (
        P("ctx", "tp"),
        P("ctx", "tp"),
        P("ctx", "tp"),
        P("ctx", "tp"),
        P("ctx", "tp"),
        P("ctx", "tp"),
        P("tp"),
        P("tp"),
        P("tp"),
        P("tp"),
        P("tp", None),
        P(),
        P(None, "tp"),
        P(),
        P("ctx"),
    )
    out_specs = (P("ctx", "tp"), P("ctx", "tp"))
    return jax.shard_map(body, mesh=mesh, in_specs=in_specs, out_specs=out_specs, check_vma=False)
```

```python
import math

import jax
import jax.numpy as jnp
from jax import lax
from jax.experimental import pallas as pl
from jax.experimental.pallas import tpu as pltpu
from jax.sharding import PartitionSpec as P

D = 2688
MHEADS = 64
HEADP = 64
STATE = 128
NGROUPS = 8
QHEADS = 32
KVHEADS = 2
HDIM = 128
MAXDOC = 6144


def fold_kernel(flag_ref, *refs, count, outs, heads, width):
    gots = refs[:count]
    curs = refs[count : count + outs]
    results = refs[count + outs :]
    base = heads * width
    for cur_ref, out_ref in zip(curs, results):
        out_ref[...] = cur_ref[...]
        for j, got_ref in enumerate(gots):

            @pl.when(flag_ref[j] > 0)
            def _():
                joined = (
                    got_ref[base + 9 : base + 10, :] == out_ref[base + 8 : base + 9, :]
                ).astype(jnp.float32)
                for h in range(heads):
                    gain = out_ref[base + h : base + h + 1, :] * joined
                    out_ref[h * width : (h + 1) * width, :] = (
                        gain * got_ref[h * width : (h + 1) * width, :]
                        + out_ref[h * width : (h + 1) * width, :]
                    )
                    out_ref[base + h : base + h + 1, :] = got_ref[base + h : base + h + 1, :] * gain
                out_ref[base + 8 : base + 9, :] = got_ref[base + 8 : base + 9, :]


def fold(flags, gots, curs, heads, width):
    vmem = pltpu.MemorySpace.VMEM
    kernel = lambda *refs: fold_kernel(
        *refs, count=len(gots), outs=len(curs), heads=heads, width=width
    )
    return pl.pallas_call(
        kernel,
        in_specs=[pl.BlockSpec(memory_space=pltpu.MemorySpace.SMEM)]
        + [pl.BlockSpec(memory_space=vmem)] * (len(gots) + len(curs)),
        out_specs=[pl.BlockSpec(memory_space=vmem)] * len(curs),
        out_shape=[jax.ShapeDtypeStruct(c.shape, c.dtype) for c in curs],
    )(flags, *gots, *curs)


def pack(decay, state, first, last):
    heads, width, size = state.shape
    meta = jnp.concatenate(
        [
            jnp.broadcast_to(decay[:, None], (heads, size)),
            jnp.full((1, size), first, jnp.float32),
            jnp.full((1, size), last, jnp.float32),
            jnp.zeros((6, size), jnp.float32),
        ],
        axis=0,
    )
    return jnp.concatenate([state.reshape(heads * width, size), meta], axis=0)


def exclusive_scan(decay, state, first, last, axis):
    peers = lax.axis_size(axis)
    position = lax.axis_index(axis)
    heads, width, size = state.shape
    assert heads == 8
    inclusive = pack(decay, state, first, last)
    before = None
    dist = 1
    while dist < peers:
        pairs = [(j, j + dist) for j in range(peers - dist)]
        sent = inclusive.astype(jnp.bfloat16)
        got = lax.ppermute(sent, axis, pairs).astype(jnp.float32)
        flags = jnp.reshape(position >= dist, (1,)).astype(jnp.int32)
        curs = [] if before is None else [before]
        if dist * 2 < peers:
            curs.append(inclusive)
        folded = fold(flags, [got], curs, heads, width) if curs else []
        if before is None:
            before = got
            if folded:
                inclusive = folded[0]
        else:
            before = folded[0]
            if len(folded) > 1:
                inclusive = folded[1]
        dist *= 2
    carried = before[: heads * width].reshape(heads, width, size)
    return carried, before[heads * width + 9, 0]


def mixer_partial(
    mamba_x, gate_z, b_input, c_input, dt_raw, dt_bias, decay_log, d_skip, mixer_gain, out_weight,
    segment,
):
    highest = lax.Precision.HIGHEST
    rows = mamba_x.shape[0]
    local_heads = dt_raw.shape[1]
    group_heads = MHEADS // NGROUPS
    local_groups = local_heads // group_heads
    position = lax.axis_index("ctx")
    segf = segment.astype(jnp.float32)
    step_size = jax.nn.softplus(dt_raw + dt_bias[None, :])
    cumulative = jnp.cumsum(-step_size * jnp.exp(decay_log)[None, :], axis=0)
    cum_heads = cumulative.T
    order = jnp.arange(rows, dtype=jnp.int32)
    same = (order[:, None] >= order[None, :]) & (segment[:, None] == segment[None, :])
    differ = jnp.where(same[None], cum_heads[:, :, None] - cum_heads[:, None, :], 0.0)
    decay_ts = jnp.where(same[None], jnp.exp(differ), 0.0) * step_size.T[:, None, :]
    heads_x = mamba_x.astype(jnp.float32).reshape(rows, local_heads, HEADP)
    groups_b = b_input.astype(jnp.float32).reshape(rows, local_groups, STATE)
    groups_c = c_input.astype(jnp.float32).reshape(rows, local_groups, STATE)
    tail = (
        jnp.exp(cumulative[-1][None, :] - cumulative)
        * (segment == segment[-1]).astype(jnp.float32)[:, None]
        * step_size
    )
    b_heads = jnp.repeat(groups_b, group_heads, axis=1)
    fresh = jnp.einsum("shp,shn->hpn", heads_x * tail[:, :, None], b_heads, precision=highest)
    whole = (segment[0] == segment[-1]).astype(jnp.float32)
    device_decay = jnp.exp(cumulative[-1]) * whole
    carried, last_before = exclusive_scan(device_decay, fresh, segf[0], segf[-1], "ctx")
    inner = jnp.einsum("tgn,sgn->gts", groups_c, groups_b, precision=highest)
    inner = jnp.repeat(inner, group_heads, axis=0)
    local_out = jnp.einsum("hts,shp->thp", inner * decay_ts, heads_x, precision=highest)
    keep = ((segf == last_before) & (position > 0)).astype(jnp.float32)
    carry_gain = jnp.exp(cumulative) * keep[:, None]
    c_heads = jnp.repeat(groups_c, group_heads, axis=1)
    carry_out = (
        jnp.einsum("thn,hpn->thp", c_heads, carried, precision=highest) * carry_gain[:, :, None]
    )
    ssm_out = local_out + carry_out + d_skip[None, :, None] * heads_x
    gated = ssm_out.reshape(rows, local_heads * HEADP) * jax.nn.silu(gate_z.astype(jnp.float32))
    grouped = gated.reshape(rows, local_groups, group_heads * HEADP)
    inv_rms = lax.rsqrt(jnp.mean(grouped * grouped, axis=2, keepdims=True) + 1e-05)
    mixed = ((grouped * inv_rms).reshape(rows, local_heads * HEADP) * mixer_gain[None, :]).astype(
        jnp.bfloat16
    )
    return jnp.dot(mixed, out_weight, preferred_element_type=jnp.float32)


def flash_kernel(where_ref, q_ref, qseg_ref, qpos_ref, *rest, window, rows, heads, width, scale):
    others = window - 1
    kv_refs = rest[:window]
    o_ref, kv_sc, sems, top_sc, total_sc, acc_sc, q_sc = rest[window:]
    position = where_ref[0]
    parity = where_ref[1]

    def distance(o):
        return o - o % 2 + 1 + jnp.bitwise_xor(o % 2, parity)

    copies = [pltpu.make_async_copy(kv_refs[b], kv_sc.at[b], sems.at[b]) for b in range(window)]
    copies[others].start()
    for o in range(others):

        @pl.when(distance(o) <= position)
        def _():
            copies[o].start()

    top_sc[...] = jnp.full(top_sc.shape, -1e30, jnp.float32)
    total_sc[...] = jnp.zeros(total_sc.shape, jnp.float32)
    acc_sc[...] = jnp.zeros(acc_sc.shape, jnp.float32)
    for h in range(heads):
        q_sc[h * rows : (h + 1) * rows, :] = q_ref[:, h * width : (h + 1) * width]

    def update(index, causal):
        q = q_sc[...]
        k = kv_sc[index, :rows, :width]
        v = kv_sc[index, :rows, width:]
        kseg = kv_sc[index, rows : rows + 1, :rows].astype(jnp.float32)
        s = lax.dot_general(q, k, (((1,), (1,)), ((), ())), preferred_element_type=jnp.float32)
        s = s * scale
        allowed = kseg == qseg_ref[...]
        if causal:
            kpos = position * rows + lax.broadcasted_iota(jnp.int32, (1, rows), 1)
            allowed = allowed & (kpos <= qpos_ref[...])
        masked = jnp.where(allowed, s, -1e30)
        top = top_sc[...]
        new_top = jnp.maximum(top, jnp.max(masked, axis=1, keepdims=True))
        p = jnp.exp(masked - new_top)
        factor = jnp.exp(top - new_top)
        total_sc[...] = total_sc[...] * factor + jnp.sum(p, axis=1, keepdims=True)
        acc_sc[...] = acc_sc[...] * factor + jnp.dot(
            p.astype(jnp.bfloat16), v, preferred_element_type=jnp.float32
        )
        top_sc[...] = new_top

    copies[others].wait()
    for o in range(others):

        @pl.when(distance(o) <= position)
        def _():
            copies[o].wait()

    update(others, True)

    def visit(o, carry):
        @pl.when(distance(o) <= position)
        def _():
            update(o, False)

        return carry

    lax.fori_loop(0, others, visit, 0)
    out = acc_sc[...] / total_sc[...]
    for h in range(heads):
        o_ref[:, h * width : (h + 1) * width] = out[h * rows : (h + 1) * rows].astype(o_ref.dtype)


def flash(where, queries, qseg, qpos, blocks, heads):
    window = len(blocks)
    rows = queries.shape[0]
    block_rows, pair = blocks[0].shape
    width = pair // 2
    kernel = lambda *refs: flash_kernel(
        *refs, window=window, rows=rows, heads=heads, width=width, scale=width ** (-0.5)
    )
    vmem = pltpu.MemorySpace.VMEM
    smem = pltpu.MemorySpace.SMEM
    return pl.pallas_call(
        kernel,
        in_specs=[pl.BlockSpec(memory_space=smem)]
        + [pl.BlockSpec(memory_space=vmem)] * 3
        + [pl.BlockSpec(memory_space=pl.ANY)] * window,
        out_specs=pl.BlockSpec(memory_space=vmem),
        out_shape=jax.ShapeDtypeStruct((rows, heads * width), jnp.bfloat16),
        scratch_shapes=[
            pltpu.VMEM((window, block_rows, pair), jnp.bfloat16),
            pltpu.SemaphoreType.DMA((window,)),
            pltpu.VMEM((heads * rows, 1), jnp.float32),
            pltpu.VMEM((heads * rows, 1), jnp.float32),
            pltpu.VMEM((heads * rows, width), jnp.float32),
            pltpu.VMEM((heads * rows, width), jnp.bfloat16),
        ],
    )(where, queries, qseg, qpos, *blocks)


def body(
    hidden, mamba_x, gate_z, b_input, c_input, dt_raw, dt_bias, decay_log, d_skip, mixer_gain,
    out_weight, attn_gain, w_query, w_keyval, segment_ids,
):
    rows, columns = hidden.shape
    peers = lax.axis_size("ctx")
    position = lax.axis_index("ctx")
    partial_out = mixer_partial(
        mamba_x, gate_z, b_input, c_input, dt_raw, dt_bias, decay_log, d_skip, mixer_gain,
        out_weight, segment_ids,
    )
    tp_index = lax.axis_index("tp")
    local_query = w_query.shape[1] // HDIM
    owner = tp_index * local_query // (QHEADS // KVHEADS)
    w_pair = lax.dynamic_index_in_dim(w_keyval, owner, 0, keepdims=False)
    own_sum = lax.psum_scatter(partial_out, "tp", scatter_dimension=1, tiled=True)
    stream = (hidden.astype(jnp.float32) + own_sum).astype(jnp.bfloat16)
    full = lax.all_gather(stream, "tp", axis=1, tiled=True).astype(jnp.float32)
    inv_rms = lax.rsqrt(jnp.sum(full * full, axis=1) / D + 1e-05)
    normed = (full * inv_rms[:, None] * attn_gain[None, :]).astype(jnp.bfloat16)
    queries = jnp.dot(normed, w_query, preferred_element_type=jnp.float32).astype(jnp.bfloat16)
    pairs = jnp.dot(normed, w_pair, preferred_element_type=jnp.float32).astype(jnp.bfloat16)
    pair_width = pairs.shape[1]
    seg_rows = jnp.zeros((16, pair_width), jnp.bfloat16)
    seg_rows = seg_rows.at[0, :rows].set(segment_ids.astype(jnp.bfloat16))
    own_block = jnp.concatenate([pairs, seg_rows], axis=0)
    back = min(peers - 1, -(-(MAXDOC - 1) // rows))
    back += back % 2
    tp_size = lax.axis_size("tp")
    assert tp_size % 2 == 0 and back < peers
    swap = [(t, t ^ 1) for t in range(tp_size)]
    blocks = []
    for near in range(1, back + 1, 2):
        pairs_list = []
        for t in range(tp_size):
            dist = near + t % 2
            pairs_list += [(j * tp_size + t, (j + dist) * tp_size + t) for j in range(peers - dist)]
        mine = lax.ppermute(own_block, ("ctx", "tp"), pairs_list)
        blocks += [mine, lax.ppermute(mine, "tp", swap)]
    blocks.append(own_block)
    heads = local_query
    qseg = jnp.tile(segment_ids.astype(jnp.float32), heads)[:, None]
    qpos = jnp.tile(position * rows + jnp.arange(rows, dtype=jnp.int32), heads)[:, None]
    where = jnp.stack([position, tp_index % 2]).astype(jnp.int32)
    context = flash(where, queries, qseg, qpos, blocks, heads)
    return (stream, context)


def solution(mesh):
    in_specs = (
        P("ctx", "tp"),
        P("ctx", "tp"),
        P("ctx", "tp"),
        P("ctx", "tp"),
        P("ctx", "tp"),
        P("ctx", "tp"),
        P("tp"),
        P("tp"),
        P("tp"),
        P("tp"),
        P("tp", None),
        P(),
        P(None, "tp"),
        P(),
        P("ctx"),
    )
    out_specs = (P("ctx", "tp"), P("ctx", "tp"))
    return jax.shard_map(body, mesh=mesh, in_specs=in_specs, out_specs=out_specs, check_vma=False)
```

```python
import math

import jax
import jax.numpy as jnp
from jax import lax
from jax.experimental import pallas as pl
from jax.experimental.pallas import tpu as pltpu
from jax.sharding import PartitionSpec as P

D = 2688
MHEADS = 64
HEADP = 64
STATE = 128
NGROUPS = 8
QHEADS = 32
KVHEADS = 2
HDIM = 128
MAXDOC = 6144


def fold_kernel(flag_ref, *refs, count, outs, heads, width):
    gots = refs[:count]
    curs = refs[count : count + outs]
    results = refs[count + outs :]
    base = heads * width
    for cur_ref, out_ref in zip(curs, results):
        out_ref[...] = cur_ref[...]
        for j, got_ref in enumerate(gots):

            @pl.when(flag_ref[j] > 0)
            def _():
                joined = (
                    got_ref[base + 9 : base + 10, :] == out_ref[base + 8 : base + 9, :]
                ).astype(jnp.float32)
                for h in range(heads):
                    gain = out_ref[base + h : base + h + 1, :] * joined
                    out_ref[h * width : (h + 1) * width, :] = (
                        gain * got_ref[h * width : (h + 1) * width, :]
                        + out_ref[h * width : (h + 1) * width, :]
                    )
                    out_ref[base + h : base + h + 1, :] = got_ref[base + h : base + h + 1, :] * gain
                out_ref[base + 8 : base + 9, :] = got_ref[base + 8 : base + 9, :]


def fold(flags, gots, curs, heads, width):
    vmem = pltpu.MemorySpace.VMEM
    kernel = lambda *refs: fold_kernel(
        *refs, count=len(gots), outs=len(curs), heads=heads, width=width
    )
    return pl.pallas_call(
        kernel,
        in_specs=[pl.BlockSpec(memory_space=pltpu.MemorySpace.SMEM)]
        + [pl.BlockSpec(memory_space=vmem)] * (len(gots) + len(curs)),
        out_specs=[pl.BlockSpec(memory_space=vmem)] * len(curs),
        out_shape=[jax.ShapeDtypeStruct(c.shape, c.dtype) for c in curs],
    )(flags, *gots, *curs)


def pack(decay, state, first, last):
    heads, width, size = state.shape
    meta = jnp.concatenate(
        [
            jnp.broadcast_to(decay[:, None], (heads, size)),
            jnp.full((1, size), first, jnp.float32),
            jnp.full((1, size), last, jnp.float32),
            jnp.zeros((6, size), jnp.float32),
        ],
        axis=0,
    )
    return jnp.concatenate([state.reshape(heads * width, size), meta], axis=0)


def exclusive_scan(decay, state, first, last, axis, need):
    peers = lax.axis_size(axis)
    position = lax.axis_index(axis)
    heads, width, size = state.shape
    assert heads == 8
    radix = 3
    inclusive = pack(decay, state, first, last)
    before = None
    base = 1
    while base - 1 < need:
        dists = [base * k for k in range(1, radix) if base * k < peers]
        gots = [
            lax.ppermute(inclusive.astype(jnp.bfloat16), axis, [(j, j + d) for j in range(peers - d)])
            .astype(jnp.float32)
            for d in dists
        ]
        flags = jnp.stack([position >= d for d in dists]).astype(jnp.int32)
        more = base * radix - 1 < need
        if before is None:
            if more:
                inclusive = fold(flags, gots, [inclusive], heads, width)[0]
            if len(gots) > 1:
                before = fold(flags[1:], gots[1:], [gots[0]], heads, width)[0]
            else:
                before = gots[0]
        else:
            curs = [before] + ([inclusive] if more else [])
            folded = fold(flags, gots, curs, heads, width)
            before = folded[0]
            if more:
                inclusive = folded[1]
        base *= radix
    carried = before[: heads * width].reshape(heads, width, size)
    return carried, before[heads * width + 9, 0]


def mixer_partial(
    mamba_x, gate_z, b_input, c_input, dt_raw, dt_bias, decay_log, d_skip, mixer_gain, out_weight,
    segment,
):
    highest = lax.Precision.HIGHEST
    rows = mamba_x.shape[0]
    local_heads = dt_raw.shape[1]
    group_heads = MHEADS // NGROUPS
    local_groups = local_heads // group_heads
    position = lax.axis_index("ctx")
    segf = segment.astype(jnp.float32)
    step_size = jax.nn.softplus(dt_raw + dt_bias[None, :])
    cumulative = jnp.cumsum(-step_size * jnp.exp(decay_log)[None, :], axis=0)
    cum_heads = cumulative.T
    order = jnp.arange(rows, dtype=jnp.int32)
    same = (order[:, None] >= order[None, :]) & (segment[:, None] == segment[None, :])
    differ = jnp.where(same[None], cum_heads[:, :, None] - cum_heads[:, None, :], 0.0)
    decay_ts = jnp.where(same[None], jnp.exp(differ), 0.0) * step_size.T[:, None, :]
    heads_x = mamba_x.astype(jnp.float32).reshape(rows, local_heads, HEADP)
    groups_b = b_input.astype(jnp.float32).reshape(rows, local_groups, STATE)
    groups_c = c_input.astype(jnp.float32).reshape(rows, local_groups, STATE)
    tail = (
        jnp.exp(cumulative[-1][None, :] - cumulative)
        * (segment == segment[-1]).astype(jnp.float32)[:, None]
        * step_size
    )
    b_heads = jnp.repeat(groups_b, group_heads, axis=1)
    fresh = jnp.einsum("shp,shn->hpn", heads_x * tail[:, :, None], b_heads, precision=highest)
    whole = (segment[0] == segment[-1]).astype(jnp.float32)
    device_decay = jnp.exp(cumulative[-1]) * whole
    need = min(lax.axis_size("ctx") - 1, (MAXDOC + rows - 2) // rows)
    carried, last_before = exclusive_scan(device_decay, fresh, segf[0], segf[-1], "ctx", need)
    inner = jnp.einsum("tgn,sgn->gts", groups_c, groups_b, precision=highest)
    inner = jnp.repeat(inner, group_heads, axis=0)
    local_out = jnp.einsum("hts,shp->thp", inner * decay_ts, heads_x, precision=highest)
    keep = ((segf == last_before) & (position > 0)).astype(jnp.float32)
    carry_gain = jnp.exp(cumulative) * keep[:, None]
    c_heads = jnp.repeat(groups_c, group_heads, axis=1)
    carry_out = (
        jnp.einsum("thn,hpn->thp", c_heads, carried, precision=highest) * carry_gain[:, :, None]
    )
    ssm_out = local_out + carry_out + d_skip[None, :, None] * heads_x
    gated = ssm_out.reshape(rows, local_heads * HEADP) * jax.nn.silu(gate_z.astype(jnp.float32))
    grouped = gated.reshape(rows, local_groups, group_heads * HEADP)
    inv_rms = lax.rsqrt(jnp.mean(grouped * grouped, axis=2, keepdims=True) + 1e-05)
    mixed = ((grouped * inv_rms).reshape(rows, local_heads * HEADP) * mixer_gain[None, :]).astype(
        jnp.bfloat16
    )
    return jnp.dot(mixed, out_weight, preferred_element_type=jnp.float32)


def flash_kernel(where_ref, q_ref, qseg_ref, qpos_ref, *rest, window, rows, heads, width, scale):
    others = window - 1
    kv_refs = rest[:window]
    o_ref, kv_sc, sems, top_sc, total_sc, acc_sc, q_sc = rest[window:]
    position = where_ref[0]
    parity = where_ref[1]

    def distance(o):
        return o - o % 2 + 1 + jnp.bitwise_xor(o % 2, parity)

    copies = [pltpu.make_async_copy(kv_refs[b], kv_sc.at[b], sems.at[b]) for b in range(window)]
    copies[others].start()
    for o in range(others):

        @pl.when(distance(o) <= position)
        def _():
            copies[o].start()

    top_sc[...] = jnp.full(top_sc.shape, -1e30, jnp.float32)
    total_sc[...] = jnp.zeros(total_sc.shape, jnp.float32)
    acc_sc[...] = jnp.zeros(acc_sc.shape, jnp.float32)
    for h in range(heads):
        q_sc[h * rows : (h + 1) * rows, :] = q_ref[:, h * width : (h + 1) * width]

    def update(index, causal):
        q = q_sc[...]
        k = kv_sc[index, :rows, :width]
        v = kv_sc[index, :rows, width:]
        kseg = kv_sc[index, rows : rows + 1, :rows].astype(jnp.float32)
        s = lax.dot_general(q, k, (((1,), (1,)), ((), ())), preferred_element_type=jnp.float32)
        s = s * scale
        allowed = kseg == qseg_ref[...]
        if causal:
            kpos = position * rows + lax.broadcasted_iota(jnp.int32, (1, rows), 1)
            allowed = allowed & (kpos <= qpos_ref[...])
        masked = jnp.where(allowed, s, -1e30)
        top = top_sc[...]
        new_top = jnp.maximum(top, jnp.max(masked, axis=1, keepdims=True))
        p = jnp.exp(masked - new_top)
        factor = jnp.exp(top - new_top)
        total_sc[...] = total_sc[...] * factor + jnp.sum(p, axis=1, keepdims=True)
        acc_sc[...] = acc_sc[...] * factor + jnp.dot(
            p.astype(jnp.bfloat16), v, preferred_element_type=jnp.float32
        )
        top_sc[...] = new_top

    copies[others].wait()
    for o in range(others):

        @pl.when(distance(o) <= position)
        def _():
            copies[o].wait()

    update(others, True)

    def visit(o, carry):
        @pl.when(distance(o) <= position)
        def _():
            update(o, False)

        return carry

    lax.fori_loop(0, others, visit, 0)
    out = acc_sc[...] / total_sc[...]
    for h in range(heads):
        o_ref[:, h * width : (h + 1) * width] = out[h * rows : (h + 1) * rows].astype(o_ref.dtype)


def flash(where, queries, qseg, qpos, blocks, heads):
    window = len(blocks)
    rows = queries.shape[0]
    block_rows, pair = blocks[0].shape
    width = pair // 2
    kernel = lambda *refs: flash_kernel(
        *refs, window=window, rows=rows, heads=heads, width=width, scale=width ** (-0.5)
    )
    vmem = pltpu.MemorySpace.VMEM
    smem = pltpu.MemorySpace.SMEM
    return pl.pallas_call(
        kernel,
        in_specs=[pl.BlockSpec(memory_space=smem)]
        + [pl.BlockSpec(memory_space=vmem)] * 3
        + [pl.BlockSpec(memory_space=pl.ANY)] * window,
        out_specs=pl.BlockSpec(memory_space=vmem),
        out_shape=jax.ShapeDtypeStruct((rows, heads * width), jnp.bfloat16),
        scratch_shapes=[
            pltpu.VMEM((window, block_rows, pair), jnp.bfloat16),
            pltpu.SemaphoreType.DMA((window,)),
            pltpu.VMEM((heads * rows, 1), jnp.float32),
            pltpu.VMEM((heads * rows, 1), jnp.float32),
            pltpu.VMEM((heads * rows, width), jnp.float32),
            pltpu.VMEM((heads * rows, width), jnp.bfloat16),
        ],
    )(where, queries, qseg, qpos, *blocks)


def body(
    hidden, mamba_x, gate_z, b_input, c_input, dt_raw, dt_bias, decay_log, d_skip, mixer_gain,
    out_weight, attn_gain, w_query, w_keyval, segment_ids,
):
    rows, columns = hidden.shape
    peers = lax.axis_size("ctx")
    position = lax.axis_index("ctx")
    partial_out = mixer_partial(
        mamba_x, gate_z, b_input, c_input, dt_raw, dt_bias, decay_log, d_skip, mixer_gain,
        out_weight, segment_ids,
    )
    tp_index = lax.axis_index("tp")
    local_query = w_query.shape[1] // HDIM
    owner = tp_index * local_query // (QHEADS // KVHEADS)
    w_pair = lax.dynamic_index_in_dim(w_keyval, owner, 0, keepdims=False)
    own_sum = lax.psum_scatter(partial_out, "tp", scatter_dimension=1, tiled=True)
    stream = (hidden.astype(jnp.float32) + own_sum).astype(jnp.bfloat16)
    full = lax.all_gather(stream, "tp", axis=1, tiled=True).astype(jnp.float32)
    inv_rms = lax.rsqrt(jnp.sum(full * full, axis=1) / D + 1e-05)
    normed = (full * inv_rms[:, None] * attn_gain[None, :]).astype(jnp.bfloat16)
    queries = jnp.dot(normed, w_query, preferred_element_type=jnp.float32).astype(jnp.bfloat16)
    pairs = jnp.dot(normed, w_pair, preferred_element_type=jnp.float32).astype(jnp.bfloat16)
    pair_width = pairs.shape[1]
    seg_rows = jnp.zeros((16, pair_width), jnp.bfloat16)
    seg_rows = seg_rows.at[0, :rows].set(segment_ids.astype(jnp.bfloat16))
    own_block = jnp.concatenate([pairs, seg_rows], axis=0)
    back = min(peers - 1, -(-(MAXDOC - 1) // rows))
    back += back % 2
    tp_size = lax.axis_size("tp")
    assert tp_size % 2 == 0 and back < peers
    swap = [(t, t ^ 1) for t in range(tp_size)]
    blocks = []
    for near in range(1, back + 1, 2):
        pairs_list = []
        for t in range(tp_size):
            dist = near + t % 2
            pairs_list += [(j * tp_size + t, (j + dist) * tp_size + t) for j in range(peers - dist)]
        mine = lax.ppermute(own_block, ("ctx", "tp"), pairs_list)
        blocks += [mine, lax.ppermute(mine, "tp", swap)]
    blocks.append(own_block)
    heads = local_query
    qseg = jnp.tile(segment_ids.astype(jnp.float32), heads)[:, None]
    qpos = jnp.tile(position * rows + jnp.arange(rows, dtype=jnp.int32), heads)[:, None]
    where = jnp.stack([position, tp_index % 2]).astype(jnp.int32)
    context = flash(where, queries, qseg, qpos, blocks, heads)
    return (stream, context)


def solution(mesh):
    in_specs = (
        P("ctx", "tp"),
        P("ctx", "tp"),
        P("ctx", "tp"),
        P("ctx", "tp"),
        P("ctx", "tp"),
        P("ctx", "tp"),
        P("tp"),
        P("tp"),
        P("tp"),
        P("tp"),
        P("tp", None),
        P(),
        P(None, "tp"),
        P(),
        P("ctx"),
    )
    out_specs = (P("ctx", "tp"), P("ctx", "tp"))
    return jax.shard_map(body, mesh=mesh, in_specs=in_specs, out_specs=out_specs, check_vma=False)
```

```python
import math

import jax
import jax.numpy as jnp
from jax import lax
from jax.experimental import pallas as pl
from jax.experimental.pallas import tpu as pltpu
from jax.sharding import PartitionSpec as P

D = 2688
MHEADS = 64
HEADP = 64
STATE = 128
NGROUPS = 8
QHEADS = 32
KVHEADS = 2
HDIM = 128
MAXDOC = 6144


def fold_kernel(flag_ref, *refs, count, outs, heads, width):
    gots = refs[:count]
    curs = refs[count : count + outs]
    results = refs[count + outs :]
    base = heads * width
    for cur_ref, out_ref in zip(curs, results):
        out_ref[...] = cur_ref[...].astype(jnp.float32)
        for j, got_ref in enumerate(gots):

            @pl.when(flag_ref[j] > 0)
            def _():
                joined = (
                    got_ref[base + 9 : base + 10, :].astype(jnp.float32) == out_ref[base + 8 : base + 9, :]
                ).astype(jnp.float32)
                for h in range(heads):
                    gain = out_ref[base + h : base + h + 1, :] * joined
                    out_ref[h * width : (h + 1) * width, :] = (
                        gain * got_ref[h * width : (h + 1) * width, :].astype(jnp.float32)
                        + out_ref[h * width : (h + 1) * width, :]
                    )
                    out_ref[base + h : base + h + 1, :] = got_ref[base + h : base + h + 1, :].astype(jnp.float32) * gain
                out_ref[base + 8 : base + 9, :] = got_ref[base + 8 : base + 9, :].astype(jnp.float32)


def fold(flags, gots, curs, heads, width):
    vmem = pltpu.MemorySpace.VMEM
    kernel = lambda *refs: fold_kernel(
        *refs, count=len(gots), outs=len(curs), heads=heads, width=width
    )
    return pl.pallas_call(
        kernel,
        in_specs=[pl.BlockSpec(memory_space=pltpu.MemorySpace.SMEM)]
        + [pl.BlockSpec(memory_space=vmem)] * (len(gots) + len(curs)),
        out_specs=[pl.BlockSpec(memory_space=vmem)] * len(curs),
        out_shape=[jax.ShapeDtypeStruct(c.shape, jnp.float32) for c in curs],
    )(flags, *gots, *curs)


def pack(decay, state, first, last):
    heads, width, size = state.shape
    meta = jnp.concatenate(
        [
            jnp.broadcast_to(decay[:, None], (heads, size)),
            jnp.full((1, size), first, jnp.float32),
            jnp.full((1, size), last, jnp.float32),
            jnp.zeros((6, size), jnp.float32),
        ],
        axis=0,
    )
    return jnp.concatenate([state.reshape(heads * width, size), meta], axis=0)


def exclusive_scan(decay, state, first, last, axis, need):
    peers = lax.axis_size(axis)
    position = lax.axis_index(axis)
    heads, width, size = state.shape
    assert heads == 8
    radix = 3
    inclusive = pack(decay, state, first, last)
    before = None
    base = 1
    while base - 1 < need:
        dists = [base * k for k in range(1, radix) if base * k < peers]
        gots = [
            lax.ppermute(inclusive.astype(jnp.bfloat16), axis, [(j, j + d) for j in range(peers - d)])
            for d in dists
        ]
        flags = jnp.stack([position >= d for d in dists]).astype(jnp.int32)
        more = base * radix - 1 < need
        if before is None:
            if more:
                inclusive = fold(flags, gots, [inclusive], heads, width)[0]
            if len(gots) > 1:
                before = fold(flags[1:], gots[1:], [gots[0]], heads, width)[0]
            else:
                before = gots[0].astype(jnp.float32)
        else:
            curs = [before] + ([inclusive] if more else [])
            folded = fold(flags, gots, curs, heads, width)
            before = folded[0]
            if more:
                inclusive = folded[1]
        base *= radix
    carried = before[: heads * width].reshape(heads, width, size)
    return carried, before[heads * width + 9, 0]


def mixer_partial(
    mamba_x, gate_z, b_input, c_input, dt_raw, dt_bias, decay_log, d_skip, mixer_gain, out_weight,
    segment,
):
    highest = lax.Precision.HIGHEST
    rows = mamba_x.shape[0]
    local_heads = dt_raw.shape[1]
    group_heads = MHEADS // NGROUPS
    local_groups = local_heads // group_heads
    position = lax.axis_index("ctx")
    segf = segment.astype(jnp.float32)
    step_size = jax.nn.softplus(dt_raw + dt_bias[None, :])
    cumulative = jnp.cumsum(-step_size * jnp.exp(decay_log)[None, :], axis=0)
    cum_heads = cumulative.T
    order = jnp.arange(rows, dtype=jnp.int32)
    same = (order[:, None] >= order[None, :]) & (segment[:, None] == segment[None, :])
    differ = jnp.where(same[None], cum_heads[:, :, None] - cum_heads[:, None, :], 0.0)
    decay_ts = jnp.where(same[None], jnp.exp(differ), 0.0) * step_size.T[:, None, :]
    heads_x = mamba_x.astype(jnp.float32).reshape(rows, local_heads, HEADP)
    groups_b = b_input.astype(jnp.float32).reshape(rows, local_groups, STATE)
    groups_c = c_input.astype(jnp.float32).reshape(rows, local_groups, STATE)
    tail = (
        jnp.exp(cumulative[-1][None, :] - cumulative)
        * (segment == segment[-1]).astype(jnp.float32)[:, None]
        * step_size
    )
    b_heads = jnp.repeat(groups_b, group_heads, axis=1)
    fresh = jnp.einsum("shp,shn->hpn", heads_x * tail[:, :, None], b_heads, precision=highest)
    whole = (segment[0] == segment[-1]).astype(jnp.float32)
    device_decay = jnp.exp(cumulative[-1]) * whole
    need = min(lax.axis_size("ctx") - 1, (MAXDOC + rows - 2) // rows)
    carried, last_before = exclusive_scan(device_decay, fresh, segf[0], segf[-1], "ctx", need)
    inner = jnp.einsum("tgn,sgn->gts", groups_c, groups_b, precision=highest)
    inner = jnp.repeat(inner, group_heads, axis=0)
    local_out = jnp.einsum("hts,shp->thp", inner * decay_ts, heads_x, precision=highest)
    keep = ((segf == last_before) & (position > 0)).astype(jnp.float32)
    carry_gain = jnp.exp(cumulative) * keep[:, None]
    c_heads = jnp.repeat(groups_c, group_heads, axis=1)
    carry_out = (
        jnp.einsum("thn,hpn->thp", c_heads, carried, precision=highest) * carry_gain[:, :, None]
    )
    ssm_out = local_out + carry_out + d_skip[None, :, None] * heads_x
    gated = ssm_out.reshape(rows, local_heads * HEADP) * jax.nn.silu(gate_z.astype(jnp.float32))
    grouped = gated.reshape(rows, local_groups, group_heads * HEADP)
    inv_rms = lax.rsqrt(jnp.mean(grouped * grouped, axis=2, keepdims=True) + 1e-05)
    mixed = ((grouped * inv_rms).reshape(rows, local_heads * HEADP) * mixer_gain[None, :]).astype(
        jnp.bfloat16
    )
    return jnp.dot(mixed, out_weight, preferred_element_type=jnp.float32)


def flash_kernel(where_ref, q_ref, qseg_ref, qpos_ref, *rest, window, rows, heads, width, scale):
    others = window - 1
    kv_refs = rest[:window]
    o_ref, kv_sc, sems, top_sc, total_sc, acc_sc, q_sc = rest[window:]
    position = where_ref[0]
    parity = where_ref[1]

    def distance(o):
        return o - o % 2 + 1 + jnp.bitwise_xor(o % 2, parity)

    copies = [pltpu.make_async_copy(kv_refs[b], kv_sc.at[b], sems.at[b]) for b in range(window)]
    copies[others].start()
    for o in range(others):

        @pl.when(distance(o) <= position)
        def _():
            copies[o].start()

    top_sc[...] = jnp.full(top_sc.shape, -1e30, jnp.float32)
    total_sc[...] = jnp.zeros(total_sc.shape, jnp.float32)
    acc_sc[...] = jnp.zeros(acc_sc.shape, jnp.float32)
    for h in range(heads):
        q_sc[h * rows : (h + 1) * rows, :] = q_ref[:, h * width : (h + 1) * width]

    def update(index, causal):
        q = q_sc[...]
        k = kv_sc[index, :rows, :width]
        v = kv_sc[index, :rows, width:]
        kseg = kv_sc[index, rows : rows + 1, :rows].astype(jnp.float32)
        s = lax.dot_general(q, k, (((1,), (1,)), ((), ())), preferred_element_type=jnp.float32)
        s = s * scale
        allowed = kseg == qseg_ref[...]
        if causal:
            kpos = position * rows + lax.broadcasted_iota(jnp.int32, (1, rows), 1)
            allowed = allowed & (kpos <= qpos_ref[...])
        masked = jnp.where(allowed, s, -1e30)
        top = top_sc[...]
        new_top = jnp.maximum(top, jnp.max(masked, axis=1, keepdims=True))
        p = jnp.exp(masked - new_top)
        factor = jnp.exp(top - new_top)
        total_sc[...] = total_sc[...] * factor + jnp.sum(p, axis=1, keepdims=True)
        acc_sc[...] = acc_sc[...] * factor + jnp.dot(
            p.astype(jnp.bfloat16), v, preferred_element_type=jnp.float32
        )
        top_sc[...] = new_top

    copies[others].wait()
    for o in range(others):

        @pl.when(distance(o) <= position)
        def _():
            copies[o].wait()

    update(others, True)

    def visit(o, carry):
        @pl.when(distance(o) <= position)
        def _():
            update(o, False)

        return carry

    lax.fori_loop(0, others, visit, 0)
    out = acc_sc[...] / total_sc[...]
    for h in range(heads):
        o_ref[:, h * width : (h + 1) * width] = out[h * rows : (h + 1) * rows].astype(o_ref.dtype)


def flash(where, queries, qseg, qpos, blocks, heads):
    window = len(blocks)
    rows = queries.shape[0]
    block_rows, pair = blocks[0].shape
    width = pair // 2
    kernel = lambda *refs: flash_kernel(
        *refs, window=window, rows=rows, heads=heads, width=width, scale=width ** (-0.5)
    )
    vmem = pltpu.MemorySpace.VMEM
    smem = pltpu.MemorySpace.SMEM
    return pl.pallas_call(
        kernel,
        in_specs=[pl.BlockSpec(memory_space=smem)]
        + [pl.BlockSpec(memory_space=vmem)] * 3
        + [pl.BlockSpec(memory_space=pl.ANY)] * window,
        out_specs=pl.BlockSpec(memory_space=vmem),
        out_shape=jax.ShapeDtypeStruct((rows, heads * width), jnp.bfloat16),
        scratch_shapes=[
            pltpu.VMEM((window, block_rows, pair), jnp.bfloat16),
            pltpu.SemaphoreType.DMA((window,)),
            pltpu.VMEM((heads * rows, 1), jnp.float32),
            pltpu.VMEM((heads * rows, 1), jnp.float32),
            pltpu.VMEM((heads * rows, width), jnp.float32),
            pltpu.VMEM((heads * rows, width), jnp.bfloat16),
        ],
    )(where, queries, qseg, qpos, *blocks)


def body(
    hidden, mamba_x, gate_z, b_input, c_input, dt_raw, dt_bias, decay_log, d_skip, mixer_gain,
    out_weight, attn_gain, w_query, w_keyval, segment_ids,
):
    rows, columns = hidden.shape
    peers = lax.axis_size("ctx")
    position = lax.axis_index("ctx")
    partial_out = mixer_partial(
        mamba_x, gate_z, b_input, c_input, dt_raw, dt_bias, decay_log, d_skip, mixer_gain,
        out_weight, segment_ids,
    )
    tp_index = lax.axis_index("tp")
    local_query = w_query.shape[1] // HDIM
    owner = tp_index * local_query // (QHEADS // KVHEADS)
    w_pair = lax.dynamic_index_in_dim(w_keyval, owner, 0, keepdims=False)
    own_sum = lax.psum_scatter(partial_out, "tp", scatter_dimension=1, tiled=True)
    stream = (hidden.astype(jnp.float32) + own_sum).astype(jnp.bfloat16)
    full = lax.all_gather(stream, "tp", axis=1, tiled=True).astype(jnp.float32)
    inv_rms = lax.rsqrt(jnp.sum(full * full, axis=1) / D + 1e-05)
    normed = (full * inv_rms[:, None] * attn_gain[None, :]).astype(jnp.bfloat16)
    queries = jnp.dot(normed, w_query, preferred_element_type=jnp.float32).astype(jnp.bfloat16)
    pairs = jnp.dot(normed, w_pair, preferred_element_type=jnp.float32).astype(jnp.bfloat16)
    pair_width = pairs.shape[1]
    seg_rows = jnp.zeros((16, pair_width), jnp.bfloat16)
    seg_rows = seg_rows.at[0, :rows].set(segment_ids.astype(jnp.bfloat16))
    own_block = jnp.concatenate([pairs, seg_rows], axis=0)
    back = min(peers - 1, -(-(MAXDOC - 1) // rows))
    back += back % 2
    tp_size = lax.axis_size("tp")
    assert tp_size % 2 == 0 and back < peers
    swap = [(t, t ^ 1) for t in range(tp_size)]
    blocks = []
    for near in range(1, back + 1, 2):
        pairs_list = []
        for t in range(tp_size):
            dist = near + t % 2
            pairs_list += [(j * tp_size + t, (j + dist) * tp_size + t) for j in range(peers - dist)]
        mine = lax.ppermute(own_block, ("ctx", "tp"), pairs_list)
        blocks += [mine, lax.ppermute(mine, "tp", swap)]
    blocks.append(own_block)
    heads = local_query
    qseg = jnp.tile(segment_ids.astype(jnp.float32), heads)[:, None]
    qpos = jnp.tile(position * rows + jnp.arange(rows, dtype=jnp.int32), heads)[:, None]
    where = jnp.stack([position, tp_index % 2]).astype(jnp.int32)
    context = flash(where, queries, qseg, qpos, blocks, heads)
    return (stream, context)


def solution(mesh):
    in_specs = (
        P("ctx", "tp"),
        P("ctx", "tp"),
        P("ctx", "tp"),
        P("ctx", "tp"),
        P("ctx", "tp"),
        P("ctx", "tp"),
        P("tp"),
        P("tp"),
        P("tp"),
        P("tp"),
        P("tp", None),
        P(),
        P(None, "tp"),
        P(),
        P("ctx"),
    )
    out_specs = (P("ctx", "tp"), P("ctx", "tp"))
    return jax.shard_map(body, mesh=mesh, in_specs=in_specs, out_specs=out_specs, check_vma=False)
```

```python
import math

import jax
import jax.numpy as jnp
from jax import lax
from jax.experimental import pallas as pl
from jax.experimental.pallas import tpu as pltpu
from jax.sharding import PartitionSpec as P

D = 2688
MHEADS = 64
HEADP = 64
STATE = 128
NGROUPS = 8
QHEADS = 32
KVHEADS = 2
HDIM = 128
MAXDOC = 6144


def fold_kernel(flag_ref, *refs, count, outs, heads, width):
    gots = refs[:count]
    curs = refs[count : count + outs]
    results = refs[count + outs :]
    base = heads * width
    for cur_ref, out_ref in zip(curs, results):
        out_ref[...] = cur_ref[...].astype(jnp.float32)
        for j, got_ref in enumerate(gots):

            @pl.when(flag_ref[j] > 0)
            def _():
                joined = (
                    got_ref[base + 9 : base + 10, :].astype(jnp.float32) == out_ref[base + 8 : base + 9, :]
                ).astype(jnp.float32)
                for h in range(heads):
                    gain = out_ref[base + h : base + h + 1, :] * joined
                    out_ref[h * width : (h + 1) * width, :] = (
                        gain * got_ref[h * width : (h + 1) * width, :].astype(jnp.float32)
                        + out_ref[h * width : (h + 1) * width, :]
                    )
                    out_ref[base + h : base + h + 1, :] = got_ref[base + h : base + h + 1, :].astype(jnp.float32) * gain
                out_ref[base + 8 : base + 9, :] = got_ref[base + 8 : base + 9, :].astype(jnp.float32)


def fold(flags, gots, curs, heads, width):
    vmem = pltpu.MemorySpace.VMEM
    kernel = lambda *refs: fold_kernel(
        *refs, count=len(gots), outs=len(curs), heads=heads, width=width
    )
    return pl.pallas_call(
        kernel,
        in_specs=[pl.BlockSpec(memory_space=pltpu.MemorySpace.SMEM)]
        + [pl.BlockSpec(memory_space=vmem)] * (len(gots) + len(curs)),
        out_specs=[pl.BlockSpec(memory_space=vmem)] * len(curs),
        out_shape=[jax.ShapeDtypeStruct(c.shape, jnp.float32) for c in curs],
    )(flags, *gots, *curs)


def pack(decay, state, first, last):
    heads, width, size = state.shape
    meta = jnp.concatenate(
        [
            jnp.broadcast_to(decay[:, None], (heads, size)),
            jnp.full((1, size), first, jnp.float32),
            jnp.full((1, size), last, jnp.float32),
            jnp.zeros((6, size), jnp.float32),
        ],
        axis=0,
    )
    return jnp.concatenate([state.reshape(heads * width, size), meta], axis=0)


def exclusive_scan(decay, state, first, last, axis, need):
    peers = lax.axis_size(axis)
    position = lax.axis_index(axis)
    heads, width, size = state.shape
    assert heads == 8
    radix = 3
    inclusive = pack(decay, state, first, last)
    before = None
    base = 1
    while base - 1 < need:
        dists = [base * k for k in range(1, radix) if base * k < peers]
        gots = [
            lax.ppermute(inclusive.astype(jnp.bfloat16), axis, [(j, j + d) for j in range(peers - d)])
            for d in dists
        ]
        flags = jnp.stack([position >= d for d in dists]).astype(jnp.int32)
        more = base * radix - 1 < need
        if before is None:
            if more:
                inclusive = fold(flags, gots, [inclusive], heads, width)[0]
            if len(gots) > 1:
                before = fold(flags[1:], gots[1:], [gots[0]], heads, width)[0]
            else:
                before = gots[0].astype(jnp.float32)
        else:
            curs = [before] + ([inclusive] if more else [])
            folded = fold(flags, gots, curs, heads, width)
            before = folded[0]
            if more:
                inclusive = folded[1]
        base *= radix
    carried = before[: heads * width].reshape(heads, width, size)
    return carried, before[heads * width + 9, 0]


def mixer_partial(
    mamba_x, gate_z, b_input, c_input, dt_raw, dt_bias, decay_log, d_skip, mixer_gain, out_weight,
    segment,
):
    highest = lax.Precision.HIGHEST
    rows = mamba_x.shape[0]
    local_heads = dt_raw.shape[1]
    group_heads = MHEADS // NGROUPS
    local_groups = local_heads // group_heads
    position = lax.axis_index("ctx")
    segf = segment.astype(jnp.float32)
    step_size = jax.nn.softplus(dt_raw + dt_bias[None, :])
    cumulative = jnp.cumsum(-step_size * jnp.exp(decay_log)[None, :], axis=0)
    cum_heads = cumulative.T
    order = jnp.arange(rows, dtype=jnp.int32)
    same = (order[:, None] >= order[None, :]) & (segment[:, None] == segment[None, :])
    differ = jnp.where(same[None], cum_heads[:, :, None] - cum_heads[:, None, :], 0.0)
    decay_ts = jnp.where(same[None], jnp.exp(differ), 0.0) * step_size.T[:, None, :]
    heads_x = mamba_x.astype(jnp.float32).reshape(rows, local_heads, HEADP)
    groups_b = b_input.astype(jnp.float32).reshape(rows, local_groups, STATE)
    groups_c = c_input.astype(jnp.float32).reshape(rows, local_groups, STATE)
    tail = (
        jnp.exp(cumulative[-1][None, :] - cumulative)
        * (segment == segment[-1]).astype(jnp.float32)[:, None]
        * step_size
    )
    b_heads = jnp.repeat(groups_b, group_heads, axis=1)
    fresh = jnp.einsum("shp,shn->hpn", heads_x * tail[:, :, None], b_heads, precision=highest)
    whole = (segment[0] == segment[-1]).astype(jnp.float32)
    device_decay = jnp.exp(cumulative[-1]) * whole
    need = min(lax.axis_size("ctx") - 1, (MAXDOC + rows - 2) // rows)
    carried, last_before = exclusive_scan(device_decay, fresh, segf[0], segf[-1], "ctx", need)
    inner = jnp.einsum("tgn,sgn->gts", groups_c, groups_b, precision=highest)
    inner = jnp.repeat(inner, group_heads, axis=0)
    local_out = jnp.einsum("hts,shp->thp", inner * decay_ts, heads_x, precision=highest)
    keep = ((segf == last_before) & (position > 0)).astype(jnp.float32)
    carry_gain = jnp.exp(cumulative) * keep[:, None]
    c_heads = jnp.repeat(groups_c, group_heads, axis=1)
    carry_out = (
        jnp.einsum("thn,hpn->thp", c_heads, carried, precision=highest) * carry_gain[:, :, None]
    )
    ssm_out = local_out + carry_out + d_skip[None, :, None] * heads_x
    gated = ssm_out.reshape(rows, local_heads * HEADP) * jax.nn.silu(gate_z.astype(jnp.float32))
    grouped = gated.reshape(rows, local_groups, group_heads * HEADP)
    inv_rms = lax.rsqrt(jnp.mean(grouped * grouped, axis=2, keepdims=True) + 1e-05)
    mixed = ((grouped * inv_rms).reshape(rows, local_heads * HEADP) * mixer_gain[None, :]).astype(
        jnp.bfloat16
    )
    return jnp.dot(mixed, out_weight, preferred_element_type=jnp.float32)


def flash_kernel(where_ref, q_ref, qseg_ref, qpos_ref, *rest, window, rows, heads, width, scale):
    others = window - 1
    kv_refs = rest[:window]
    o_ref, kv_sc, sems, top_sc, total_sc, acc_sc, q_sc = rest[window:]
    position = where_ref[0]
    parity = where_ref[1]

    def distance(o):
        return o - o % 2 + 1 + jnp.bitwise_xor(o % 2, parity)

    copies = [pltpu.make_async_copy(kv_refs[b], kv_sc.at[b], sems.at[b]) for b in range(window)]
    copies[others].start()
    for o in range(others):

        @pl.when(distance(o) <= position)
        def _():
            copies[o].start()

    top_sc[...] = jnp.full(top_sc.shape, -1e30, jnp.float32)
    total_sc[...] = jnp.zeros(total_sc.shape, jnp.float32)
    acc_sc[...] = jnp.zeros(acc_sc.shape, jnp.float32)
    for h in range(heads):
        q_sc[h * rows : (h + 1) * rows, :] = q_ref[:, h * width : (h + 1) * width]

    def update(index, causal):
        k = kv_sc[index, :rows, :width]
        v = kv_sc[index, :rows, width:]
        kseg_row = kv_sc[index, rows : rows + 1, :rows].astype(jnp.float32)
        kseg = jnp.transpose(jnp.broadcast_to(kseg_row, (width, rows)))[:, :1]
        s = lax.dot_general(k, q_sc[...], (((1,), (1,)), ((), ())), preferred_element_type=jnp.float32)
        s = s * scale
        allowed = kseg == qseg_ref[...]
        if causal:
            kpos = position * rows + lax.broadcasted_iota(jnp.int32, (rows, 1), 0)
            allowed = allowed & (kpos <= qpos_ref[...])
        masked = jnp.where(allowed, s, -1e30)
        top = top_sc[...]
        new_top = jnp.maximum(top, jnp.max(masked, axis=0, keepdims=True))
        p = jnp.exp(masked - new_top)
        factor = jnp.exp(top - new_top)
        total_sc[...] = total_sc[...] * factor + jnp.sum(p, axis=0, keepdims=True)
        v_t = jnp.transpose(v.astype(jnp.float32)).astype(jnp.bfloat16)
        acc_sc[...] = acc_sc[...] * factor + jnp.dot(
            v_t, p.astype(jnp.bfloat16), preferred_element_type=jnp.float32
        )
        top_sc[...] = new_top

    copies[others].wait()
    for o in range(others):

        @pl.when(distance(o) <= position)
        def _():
            copies[o].wait()

    update(others, True)

    def visit(o, carry):
        @pl.when(distance(o) <= position)
        def _():
            update(o, False)

        return carry

    lax.fori_loop(0, others, visit, 0)
    out = jnp.transpose(acc_sc[...] / total_sc[...])
    for h in range(heads):
        o_ref[:, h * width : (h + 1) * width] = out[h * rows : (h + 1) * rows].astype(o_ref.dtype)


def flash(where, queries, qseg, qpos, blocks, heads):
    window = len(blocks)
    rows = queries.shape[0]
    block_rows, pair = blocks[0].shape
    width = pair // 2
    kernel = lambda *refs: flash_kernel(
        *refs, window=window, rows=rows, heads=heads, width=width, scale=width ** (-0.5)
    )
    vmem = pltpu.MemorySpace.VMEM
    smem = pltpu.MemorySpace.SMEM
    return pl.pallas_call(
        kernel,
        in_specs=[pl.BlockSpec(memory_space=smem)]
        + [pl.BlockSpec(memory_space=vmem)] * 3
        + [pl.BlockSpec(memory_space=pl.ANY)] * window,
        out_specs=pl.BlockSpec(memory_space=vmem),
        out_shape=jax.ShapeDtypeStruct((rows, heads * width), jnp.bfloat16),
        scratch_shapes=[
            pltpu.VMEM((window, block_rows, pair), jnp.bfloat16),
            pltpu.SemaphoreType.DMA((window,)),
            pltpu.VMEM((1, heads * rows), jnp.float32),
            pltpu.VMEM((1, heads * rows), jnp.float32),
            pltpu.VMEM((width, heads * rows), jnp.float32),
            pltpu.VMEM((heads * rows, width), jnp.bfloat16),
        ],
    )(where, queries, qseg, qpos, *blocks)


def body(
    hidden, mamba_x, gate_z, b_input, c_input, dt_raw, dt_bias, decay_log, d_skip, mixer_gain,
    out_weight, attn_gain, w_query, w_keyval, segment_ids,
):
    rows, columns = hidden.shape
    peers = lax.axis_size("ctx")
    position = lax.axis_index("ctx")
    partial_out = mixer_partial(
        mamba_x, gate_z, b_input, c_input, dt_raw, dt_bias, decay_log, d_skip, mixer_gain,
        out_weight, segment_ids,
    )
    tp_index = lax.axis_index("tp")
    local_query = w_query.shape[1] // HDIM
    owner = tp_index * local_query // (QHEADS // KVHEADS)
    w_pair = lax.dynamic_index_in_dim(w_keyval, owner, 0, keepdims=False)
    own_sum = lax.psum_scatter(partial_out, "tp", scatter_dimension=1, tiled=True)
    stream = (hidden.astype(jnp.float32) + own_sum).astype(jnp.bfloat16)
    full = lax.all_gather(stream, "tp", axis=1, tiled=True).astype(jnp.float32)
    inv_rms = lax.rsqrt(jnp.sum(full * full, axis=1) / D + 1e-05)
    normed = (full * inv_rms[:, None] * attn_gain[None, :]).astype(jnp.bfloat16)
    queries = jnp.dot(normed, w_query, preferred_element_type=jnp.float32).astype(jnp.bfloat16)
    pairs = jnp.dot(normed, w_pair, preferred_element_type=jnp.float32).astype(jnp.bfloat16)
    pair_width = pairs.shape[1]
    seg_rows = jnp.zeros((16, pair_width), jnp.bfloat16)
    seg_rows = seg_rows.at[0, :rows].set(segment_ids.astype(jnp.bfloat16))
    own_block = jnp.concatenate([pairs, seg_rows], axis=0)
    back = min(peers - 1, -(-(MAXDOC - 1) // rows))
    back += back % 2
    tp_size = lax.axis_size("tp")
    assert tp_size % 2 == 0 and back < peers
    swap = [(t, t ^ 1) for t in range(tp_size)]
    blocks = []
    for near in range(1, back + 1, 2):
        pairs_list = []
        for t in range(tp_size):
            dist = near + t % 2
            pairs_list += [(j * tp_size + t, (j + dist) * tp_size + t) for j in range(peers - dist)]
        mine = lax.ppermute(own_block, ("ctx", "tp"), pairs_list)
        blocks += [mine, lax.ppermute(mine, "tp", swap)]
    blocks.append(own_block)
    heads = local_query
    qseg = jnp.tile(segment_ids.astype(jnp.float32), heads)[None, :]
    qpos = jnp.tile(position * rows + jnp.arange(rows, dtype=jnp.int32), heads)[None, :]
    where = jnp.stack([position, tp_index % 2]).astype(jnp.int32)
    context = flash(where, queries, qseg, qpos, blocks, heads)
    return (stream, context)


def solution(mesh):
    in_specs = (
        P("ctx", "tp"),
        P("ctx", "tp"),
        P("ctx", "tp"),
        P("ctx", "tp"),
        P("ctx", "tp"),
        P("ctx", "tp"),
        P("tp"),
        P("tp"),
        P("tp"),
        P("tp"),
        P("tp", None),
        P(),
        P(None, "tp"),
        P(),
        P("ctx"),
    )
    out_specs = (P("ctx", "tp"), P("ctx", "tp"))
    return jax.shard_map(body, mesh=mesh, in_specs=in_specs, out_specs=out_specs, check_vma=False)
```

```python
import math

import jax
import jax.numpy as jnp
from jax import lax
from jax.experimental import pallas as pl
from jax.experimental.pallas import tpu as pltpu
from jax.sharding import PartitionSpec as P

D = 2688
MHEADS = 64
HEADP = 64
STATE = 128
NGROUPS = 8
QHEADS = 32
KVHEADS = 2
HDIM = 128
MAXDOC = 6144


def fold_kernel(flag_ref, *refs, count, outs, heads, width):
    gots = refs[:count]
    curs = refs[count : count + outs]
    results = refs[count + outs :]
    base = heads * width
    for cur_ref, out_ref in zip(curs, results):
        out_ref[...] = cur_ref[...].astype(jnp.float32)
        for j, got_ref in enumerate(gots):

            @pl.when(flag_ref[j] > 0)
            def _():
                joined = (
                    got_ref[base + 9 : base + 10, :].astype(jnp.float32) == out_ref[base + 8 : base + 9, :]
                ).astype(jnp.float32)
                for h in range(heads):
                    gain = out_ref[base + h : base + h + 1, :] * joined
                    out_ref[h * width : (h + 1) * width, :] = (
                        gain * got_ref[h * width : (h + 1) * width, :].astype(jnp.float32)
                        + out_ref[h * width : (h + 1) * width, :]
                    )
                    out_ref[base + h : base + h + 1, :] = got_ref[base + h : base + h + 1, :].astype(jnp.float32) * gain
                out_ref[base + 8 : base + 9, :] = got_ref[base + 8 : base + 9, :].astype(jnp.float32)


def fold(flags, gots, curs, heads, width):
    vmem = pltpu.MemorySpace.VMEM
    kernel = lambda *refs: fold_kernel(
        *refs, count=len(gots), outs=len(curs), heads=heads, width=width
    )
    return pl.pallas_call(
        kernel,
        in_specs=[pl.BlockSpec(memory_space=pltpu.MemorySpace.SMEM)]
        + [pl.BlockSpec(memory_space=vmem)] * (len(gots) + len(curs)),
        out_specs=[pl.BlockSpec(memory_space=vmem)] * len(curs),
        out_shape=[jax.ShapeDtypeStruct(c.shape, jnp.float32) for c in curs],
    )(flags, *gots, *curs)


def pack(decay, state, first, last):
    heads, width, size = state.shape
    meta = jnp.concatenate(
        [
            jnp.broadcast_to(decay[:, None], (heads, size)),
            jnp.full((1, size), first, jnp.float32),
            jnp.full((1, size), last, jnp.float32),
            jnp.zeros((6, size), jnp.float32),
        ],
        axis=0,
    )
    return jnp.concatenate([state.reshape(heads * width, size), meta], axis=0)


def exclusive_scan(decay, state, first, last, axis, need):
    peers = lax.axis_size(axis)
    position = lax.axis_index(axis)
    heads, width, size = state.shape
    assert heads == 8
    radix = 3
    inclusive = pack(decay, state, first, last)
    before = None
    base = 1
    while base - 1 < need:
        dists = [base * k for k in range(1, radix) if base * k < peers]
        gots = [
            lax.ppermute(inclusive.astype(jnp.bfloat16), axis, [(j, j + d) for j in range(peers - d)])
            for d in dists
        ]
        flags = jnp.stack([position >= d for d in dists]).astype(jnp.int32)
        more = base * radix - 1 < need
        if before is None:
            if more:
                inclusive = fold(flags, gots, [inclusive], heads, width)[0]
            if len(gots) > 1:
                before = fold(flags[1:], gots[1:], [gots[0]], heads, width)[0]
            else:
                before = gots[0].astype(jnp.float32)
        else:
            curs = [before] + ([inclusive] if more else [])
            folded = fold(flags, gots, curs, heads, width)
            before = folded[0]
            if more:
                inclusive = folded[1]
        base *= radix
    carried = before[: heads * width].reshape(heads, width, size)
    return carried, before[heads * width + 9, 0]


def mixer_partial(
    mamba_x, gate_z, b_input, c_input, dt_raw, dt_bias, decay_log, d_skip, mixer_gain, out_weight,
    segment,
):
    highest = lax.Precision.HIGHEST
    rows = mamba_x.shape[0]
    local_heads = dt_raw.shape[1]
    group_heads = MHEADS // NGROUPS
    local_groups = local_heads // group_heads
    position = lax.axis_index("ctx")
    segf = segment.astype(jnp.float32)
    step_size = jax.nn.softplus(dt_raw + dt_bias[None, :])
    cumulative = jnp.cumsum(-step_size * jnp.exp(decay_log)[None, :], axis=0)
    cum_heads = cumulative.T
    order = jnp.arange(rows, dtype=jnp.int32)
    same = (order[:, None] >= order[None, :]) & (segment[:, None] == segment[None, :])
    differ = jnp.where(same[None], cum_heads[:, :, None] - cum_heads[:, None, :], 0.0)
    decay_ts = jnp.where(same[None], jnp.exp(differ), 0.0) * step_size.T[:, None, :]
    heads_x = mamba_x.astype(jnp.float32).reshape(rows, local_heads, HEADP)
    groups_b = b_input.astype(jnp.float32).reshape(rows, local_groups, STATE)
    groups_c = c_input.astype(jnp.float32).reshape(rows, local_groups, STATE)
    tail = (
        jnp.exp(cumulative[-1][None, :] - cumulative)
        * (segment == segment[-1]).astype(jnp.float32)[:, None]
        * step_size
    )
    b_heads = jnp.repeat(groups_b, group_heads, axis=1)
    fresh = jnp.einsum("shp,shn->hpn", heads_x * tail[:, :, None], b_heads, precision=highest)
    whole = (segment[0] == segment[-1]).astype(jnp.float32)
    device_decay = jnp.exp(cumulative[-1]) * whole
    need = min(lax.axis_size("ctx") - 1, (MAXDOC + rows - 2) // rows)
    carried, last_before = exclusive_scan(device_decay, fresh, segf[0], segf[-1], "ctx", need)
    inner = jnp.einsum("tgn,sgn->gts", groups_c, groups_b, precision=highest)
    inner = jnp.repeat(inner, group_heads, axis=0)
    local_out = jnp.einsum("hts,shp->thp", inner * decay_ts, heads_x, precision=highest)
    keep = ((segf == last_before) & (position > 0)).astype(jnp.float32)
    carry_gain = jnp.exp(cumulative) * keep[:, None]
    c_heads = jnp.repeat(groups_c, group_heads, axis=1)
    carry_out = (
        jnp.einsum("thn,hpn->thp", c_heads, carried, precision=highest) * carry_gain[:, :, None]
    )
    ssm_out = local_out + carry_out + d_skip[None, :, None] * heads_x
    gated = ssm_out.reshape(rows, local_heads * HEADP) * jax.nn.silu(gate_z.astype(jnp.float32))
    grouped = gated.reshape(rows, local_groups, group_heads * HEADP)
    inv_rms = lax.rsqrt(jnp.mean(grouped * grouped, axis=2, keepdims=True) + 1e-05)
    mixed = ((grouped * inv_rms).reshape(rows, local_heads * HEADP) * mixer_gain[None, :]).astype(
        jnp.bfloat16
    )
    return jnp.dot(mixed, out_weight, preferred_element_type=jnp.float32)


def flash_kernel(where_ref, q_ref, qseg_ref, qpos_ref, *rest, window, rows, heads, width, scale):
    others = window - 1
    kv_refs = rest[:window]
    o_ref, kv_sc, sems, top_sc, total_sc, acc_sc, q_sc = rest[window:]
    position = where_ref[0]
    parity = where_ref[1]

    def distance(o):
        return o - o % 2 + 1 + jnp.bitwise_xor(o % 2, parity)

    copies = [pltpu.make_async_copy(kv_refs[b], kv_sc.at[b], sems.at[b]) for b in range(window)]
    copies[others].start()
    for o in range(others):

        @pl.when(distance(o) <= position)
        def _():
            copies[o].start()

    top_sc[...] = jnp.full(top_sc.shape, -1e30, jnp.float32)
    total_sc[...] = jnp.zeros(total_sc.shape, jnp.float32)
    acc_sc[...] = jnp.zeros(acc_sc.shape, jnp.float32)
    for h in range(heads):
        q_sc[h * rows : (h + 1) * rows, :] = q_ref[:, h * width : (h + 1) * width]

    def update(index, causal):
        k = kv_sc[index, :rows, :width]
        v_t = jnp.concatenate(
            [kv_sc[index, :width, width:], kv_sc[index, width : 2 * width, width:]], axis=1
        )
        kseg_row = kv_sc[index, rows : rows + 1, :rows].astype(jnp.float32)
        kseg = jnp.transpose(jnp.broadcast_to(kseg_row, (width, rows)))[:, :1]
        s = lax.dot_general(k, q_sc[...], (((1,), (1,)), ((), ())), preferred_element_type=jnp.float32)
        s = s * scale
        allowed = kseg == qseg_ref[...]
        if causal:
            kpos = position * rows + lax.broadcasted_iota(jnp.int32, (rows, 1), 0)
            allowed = allowed & (kpos <= qpos_ref[...])
        masked = jnp.where(allowed, s, -1e30)
        top = top_sc[...]
        new_top = jnp.maximum(top, jnp.max(masked, axis=0, keepdims=True))
        p = jnp.exp(masked - new_top)
        factor = jnp.exp(top - new_top)
        total_sc[...] = total_sc[...] * factor + jnp.sum(p, axis=0, keepdims=True)
        acc_sc[...] = acc_sc[...] * factor + jnp.dot(
            v_t, p.astype(jnp.bfloat16), preferred_element_type=jnp.float32
        )
        top_sc[...] = new_top

    copies[others].wait()
    for o in range(others):

        @pl.when(distance(o) <= position)
        def _():
            copies[o].wait()

    update(others, True)

    def visit(o, carry):
        @pl.when(distance(o) <= position)
        def _():
            update(o, False)

        return carry

    lax.fori_loop(0, others, visit, 0)
    out = jnp.transpose(acc_sc[...] / total_sc[...])
    for h in range(heads):
        o_ref[:, h * width : (h + 1) * width] = out[h * rows : (h + 1) * rows].astype(o_ref.dtype)


def flash(where, queries, qseg, qpos, blocks, heads):
    window = len(blocks)
    rows = queries.shape[0]
    block_rows, pair = blocks[0].shape
    width = pair // 2
    kernel = lambda *refs: flash_kernel(
        *refs, window=window, rows=rows, heads=heads, width=width, scale=width ** (-0.5)
    )
    vmem = pltpu.MemorySpace.VMEM
    smem = pltpu.MemorySpace.SMEM
    return pl.pallas_call(
        kernel,
        in_specs=[pl.BlockSpec(memory_space=smem)]
        + [pl.BlockSpec(memory_space=vmem)] * 3
        + [pl.BlockSpec(memory_space=pl.ANY)] * window,
        out_specs=pl.BlockSpec(memory_space=vmem),
        out_shape=jax.ShapeDtypeStruct((rows, heads * width), jnp.bfloat16),
        scratch_shapes=[
            pltpu.VMEM((window, block_rows, pair), jnp.bfloat16),
            pltpu.SemaphoreType.DMA((window,)),
            pltpu.VMEM((1, heads * rows), jnp.float32),
            pltpu.VMEM((1, heads * rows), jnp.float32),
            pltpu.VMEM((width, heads * rows), jnp.float32),
            pltpu.VMEM((heads * rows, width), jnp.bfloat16),
        ],
    )(where, queries, qseg, qpos, *blocks)


def body(
    hidden, mamba_x, gate_z, b_input, c_input, dt_raw, dt_bias, decay_log, d_skip, mixer_gain,
    out_weight, attn_gain, w_query, w_keyval, segment_ids,
):
    rows, columns = hidden.shape
    peers = lax.axis_size("ctx")
    position = lax.axis_index("ctx")
    partial_out = mixer_partial(
        mamba_x, gate_z, b_input, c_input, dt_raw, dt_bias, decay_log, d_skip, mixer_gain,
        out_weight, segment_ids,
    )
    tp_index = lax.axis_index("tp")
    local_query = w_query.shape[1] // HDIM
    owner = tp_index * local_query // (QHEADS // KVHEADS)
    w_pair = lax.dynamic_index_in_dim(w_keyval, owner, 0, keepdims=False)
    own_sum = lax.psum_scatter(partial_out, "tp", scatter_dimension=1, tiled=True)
    stream = (hidden.astype(jnp.float32) + own_sum).astype(jnp.bfloat16)
    full = lax.all_gather(stream, "tp", axis=1, tiled=True).astype(jnp.float32)
    inv_rms = lax.rsqrt(jnp.sum(full * full, axis=1) / D + 1e-05)
    normed = (full * inv_rms[:, None] * attn_gain[None, :]).astype(jnp.bfloat16)
    queries = jnp.dot(normed, w_query, preferred_element_type=jnp.float32).astype(jnp.bfloat16)
    pairs = jnp.dot(normed, w_pair, preferred_element_type=jnp.float32).astype(jnp.bfloat16)
    pair_width = pairs.shape[1]
    assert pair_width == 2 * HDIM and rows == 2 * HDIM
    values_t = pairs[:, HDIM:].T
    pairs = jnp.concatenate(
        [pairs[:, :HDIM], jnp.concatenate([values_t[:, :HDIM], values_t[:, HDIM:]], axis=0)], axis=1
    )
    seg_rows = jnp.zeros((16, pair_width), jnp.bfloat16)
    seg_rows = seg_rows.at[0, :rows].set(segment_ids.astype(jnp.bfloat16))
    own_block = jnp.concatenate([pairs, seg_rows], axis=0)
    back = min(peers - 1, -(-(MAXDOC - 1) // rows))
    back += back % 2
    tp_size = lax.axis_size("tp")
    assert tp_size % 2 == 0 and back < peers
    swap = [(t, t ^ 1) for t in range(tp_size)]
    blocks = []
    for near in range(1, back + 1, 2):
        pairs_list = []
        for t in range(tp_size):
            dist = near + t % 2
            pairs_list += [(j * tp_size + t, (j + dist) * tp_size + t) for j in range(peers - dist)]
        mine = lax.ppermute(own_block, ("ctx", "tp"), pairs_list)
        blocks += [mine, lax.ppermute(mine, "tp", swap)]
    blocks.append(own_block)
    heads = local_query
    qseg = jnp.tile(segment_ids.astype(jnp.float32), heads)[None, :]
    qpos = jnp.tile(position * rows + jnp.arange(rows, dtype=jnp.int32), heads)[None, :]
    where = jnp.stack([position, tp_index % 2]).astype(jnp.int32)
    context = flash(where, queries, qseg, qpos, blocks, heads)
    return (stream, context)


def solution(mesh):
    in_specs = (
        P("ctx", "tp"),
        P("ctx", "tp"),
        P("ctx", "tp"),
        P("ctx", "tp"),
        P("ctx", "tp"),
        P("ctx", "tp"),
        P("tp"),
        P("tp"),
        P("tp"),
        P("tp"),
        P("tp", None),
        P(),
        P(None, "tp"),
        P(),
        P("ctx"),
    )
    out_specs = (P("ctx", "tp"), P("ctx", "tp"))
    return jax.shard_map(body, mesh=mesh, in_specs=in_specs, out_specs=out_specs, check_vma=False)
```
